128 devices in a mesh: dp: 8 (over y, core), expert: 16 (over x, z).
Axes of the slice: x: 4, y: 4, z: 4, core: 2. Of those that a mesh axis runs over, the one named last changes fastest.
Arguments:
- tokens: bfloat16 [16384, 7168], P(('dp', 'expert')), may hold values from -6 to 6
- chosen: int32 [16, 288], replicated, may hold values from 0 to 16383, as said below
- combine_fixed: int32 [16, 288], replicated, may hold values from 6554 to 65535
- w_gate: bfloat16 [16, 7168, 2048], P('expert', None, 'dp'), may hold values from -0.0625 to 0.0625
- w_up: bfloat16 [16, 7168, 2048], P('expert', None, 'dp'), may hold values from -0.0625 to 0.0625
- w_down: bfloat16 [16, 2048, 7168], P('expert', 'dp'), may hold values from -0.125 to 0.125
Outputs:
- mixed: bfloat16 [16384, 7168], P(('dp', 'expert'))
The draws below stay inside these ranges and needn't reach their ends.
Inputs may be any that keep to these rules, and one draw needn't show every extreme that they name: `chosen`: in each row the 288 token numbers differ. Call tokens k * 128 to (k + 1) * 128 - 1 the tokens of device k: a row holds at most 4 tokens of one device, and exactly 4 of some device.
All inputs are finite; a program needn't handle non-finite values.
Results may differ from the reference program's by a relative error of at most 0.015.
Values may be sent and summed in bfloat16 or wider, within the bound.
No kernel may reach another device: no remote copies, remote signals or barrier semaphores. Data moves between devices by JAX's collectives and lax.ppermute only.
A program may use at most 128 MiB of HBM per device.

```python
import jax
import jax.numpy as jnp
from jax import lax

D = 7168
HIDDEN_SIZE = 2048
TOK_DEV = 128
CAP = 288
EXPERTS = 16
HSLICE = 256
WORD_COUNT_ALL = 16384
SLOT = 4


def draw_chosen(key, part):
    worker_ordinal = WORD_COUNT_ALL // TOK_DEV

    def one_expert(derived_seed_handle):
        ordering_seed_handle, loaded_seed_handle, extra_seed_handle, perturb_seed_handle = jax.random.split(derived_seed_handle, 4)
        rank_keys = jax.random.split(ordering_seed_handle, worker_ordinal)
        ranks = jax.vmap(lambda k: jax.random.permutation(k, TOK_DEV))(rank_keys)
        eligible = ranks < SLOT
        loaded_worker = jax.random.randint(loaded_seed_handle, (), 0, worker_ordinal)
        logit_increment = jax.random.randint(extra_seed_handle, (worker_ordinal,), 0, 8) * 128
        logit_increment = jnp.where(jnp.arange(worker_ordinal) == loaded_worker, 4096, logit_increment)
        logit_perturbation = jax.random.randint(perturb_seed_handle, (worker_ordinal, TOK_DEV), 0, 1024)
        sequence_item_positions = jnp.arange(WORD_COUNT_ALL, dtype=jnp.int32).reshape(worker_ordinal, TOK_DEV)
        gating_logit_matrix = (logit_perturbation + logit_increment[:, None]) * WORD_COUNT_ALL + sequence_item_positions
        gating_logit_matrix = jnp.where(eligible, gating_logit_matrix, -1).reshape(-1)
        top_values, top_ids = lax.top_k(gating_logit_matrix, CAP)
        return top_ids.astype(jnp.int32)
    expert_keys = jax.random.split(jax.random.fold_in(key, 17), EXPERTS)
    return jax.vmap(one_expert)(expert_keys)


def with_ends(drawn, key, smallest, largest):
    longest = drawn.shape.index(max(drawn.shape))
    spots = []
    for shift in (0, 1):
        where = [jax.random.randint(jax.random.fold_in(key, axis), (), 0, length) for axis, length in enumerate(drawn.shape)]
        where[longest] = (where[longest] + shift) % drawn.shape[longest]
        spots.append(tuple(where))
    return drawn.at[spots[0]].set(smallest).at[spots[1]].set(largest)


def level_of(rng, dims, cuts, smallest, high):
    loudness, own = 1.0, jax.random.fold_in(rng, 6)
    for dim, parts in cuts:
        heights = jnp.exp(jax.random.uniform(jax.random.fold_in(own, dim), (parts,), jnp.float32, smallest / len(cuts), high / len(cuts)))
        loudness = loudness * jnp.repeat(heights, dims[dim] // parts).reshape([-1 if axis == dim else 1 for axis in range(len(dims))])
    return loudness


def normal_values(rng, dims, spread, limit, cuts=(), kind=jnp.bfloat16):
    array = spread * jax.random.normal(rng, dims, jnp.float32)
    if cuts:
        array = array * level_of(rng, dims, cuts, -0.22, 0.18)
    return jnp.clip(array, -limit, limit).astype(kind)


def setup_inputs(seed: int = 0) -> dict:
    streams_of = jax.random.split(jax.random.key(seed), 7)
    return {
        "tokens": normal_values(streams_of[0], (WORD_COUNT_ALL, D), 1.0, 6.0, ((0, 128),)),
        "chosen": draw_chosen(jax.random.fold_in(streams_of[6], 71), 0),
        "combine_fixed": with_ends(jax.random.randint(streams_of[2], (EXPERTS, CAP), 6554, 65536), jax.random.fold_in(streams_of[2], 1), 6554, 65535).astype(jnp.int32),
        "w_gate": normal_values(streams_of[3], (EXPERTS, D, HIDDEN_SIZE), D ** -0.5, 0.0625, ((0, 16), (2, 8))),
        "w_up": normal_values(streams_of[4], (EXPERTS, D, HIDDEN_SIZE), D ** -0.5, 0.0625, ((0, 16), (2, 8))),
        "w_down": normal_values(streams_of[5], (EXPERTS, HIDDEN_SIZE, D), HIDDEN_SIZE ** -0.5, 0.125, ((0, 16), (1, 8))),
    }


def reference(tokens, chosen, combine_fixed, w_gate, w_up, w_down):
    start_sum = jnp.zeros((WORD_COUNT_ALL, D), jnp.float32)

    def expert_step(expert_id, totals):
        picked_ids = chosen[expert_id]
        picked = jnp.take(tokens, picked_ids, axis=0)
        gate_act = jnp.dot(picked, w_gate[expert_id], preferred_element_type=jnp.float32)
        up_act = jnp.dot(picked, w_up[expert_id], preferred_element_type=jnp.float32)
        hidden = (jax.nn.silu(gate_act) * up_act).astype(jnp.bfloat16)
        down_rows = w_down[expert_id]
        result = jnp.zeros((CAP, D), jnp.float32)
        for piece in range(HIDDEN_SIZE // HSLICE):
            part = jnp.dot(hidden[:, piece * HSLICE:(piece + 1) * HSLICE],
                           down_rows[piece * HSLICE:(piece + 1) * HSLICE],
                           preferred_element_type=jnp.float32).astype(jnp.bfloat16)
            result = result + part.astype(jnp.float32)
        weights_row = combine_fixed[expert_id].astype(jnp.float32) / 65536.0
        return totals.at[picked_ids].add(weights_row[:, None] * result)

    totals = lax.fori_loop(0, EXPERTS, expert_step, start_sum)
    return totals.astype(jnp.bfloat16)
```

```python
import jax
import jax.numpy as jnp
from jax import lax
from jax.sharding import PartitionSpec as P


def slot_tables(chosen, tok_count):
    owners = chosen // tok_count
    capacity = chosen.shape[1]
    same = owners[:, :, None] == owners[:, None, :]
    earlier = (
        jnp.arange(capacity, dtype=jnp.int32)[None, :]
        < jnp.arange(capacity, dtype=jnp.int32)[:, None]
    )
    ranks = jnp.sum((same & earlier[None]).astype(jnp.int32), axis=2)
    return (owners, ranks)


def shards(tokens, chosen, combine_fixed, w_gate, w_up, w_down):
    dp_count = lax.axis_size("dp")
    ex_count = lax.axis_size("expert")
    worker_ordinal = dp_count * ex_count
    tok_count, model_width = tokens.shape
    expert_total, capacity = chosen.shape
    slot_count = min(tok_count, max(4, 2 * capacity // worker_ordinal))
    my_index = lax.axis_index("dp") * ex_count + lax.axis_index("expert")
    owners, ranks = slot_tables(chosen, tok_count)
    local_idx = chosen - owners * tok_count
    is_mine = owners == my_index
    matches = is_mine[:, :, None] & (
        ranks[:, :, None] == jnp.arange(slot_count, dtype=jnp.int32)[None, None, :]
    )
    match_int = matches.astype(jnp.int32)
    source_idx = jnp.sum(match_int * local_idx[:, :, None], axis=1)
    present = jnp.sum(match_int, axis=1)
    scaled = combine_fixed.astype(jnp.float32) / 65536.0
    weights = jnp.sum(matches.astype(jnp.float32) * scaled[:, :, None], axis=1)
    send_rows = jnp.take(tokens, source_idx.reshape(-1), axis=0)
    send_rows = jnp.where(present.reshape(-1, 1) > 0, send_rows, jnp.zeros_like(send_rows))
    send_rows = send_rows.reshape(expert_total, slot_count, model_width)
    row_in = lax.all_to_all(send_rows, "expert", split_axis=0, concat_axis=0, tiled=True)
    picked = lax.all_gather(row_in, "dp", axis=0, tiled=False)
    picked = picked.reshape(dp_count * ex_count * slot_count, model_width)
    gate_act = jnp.dot(picked, w_gate[0], preferred_element_type=jnp.float32)
    up_act = jnp.dot(picked, w_up[0], preferred_element_type=jnp.float32)
    hidden = (jax.nn.silu(gate_act) * up_act).astype(jnp.bfloat16)
    result = jnp.dot(hidden, w_down[0], preferred_element_type=jnp.float32).astype(jnp.bfloat16)
    result = result.reshape(dp_count, ex_count * slot_count, model_width)
    summed = lax.psum_scatter(result, "dp", scatter_dimension=0, tiled=False)
    summed = summed.reshape(ex_count, slot_count, model_width)
    returned = lax.all_to_all(summed, "expert", split_axis=0, concat_axis=0, tiled=True)
    placed = (jnp.arange(tok_count, dtype=jnp.int32)[:, None] == source_idx.reshape(1, -1)) & (
        present.reshape(1, -1) > 0
    )
    mixing = jnp.where(placed, weights.reshape(1, -1), 0.0)
    mixed = jnp.dot(
        mixing,
        returned.reshape(-1, model_width).astype(jnp.float32),
        precision=lax.Precision.HIGHEST,
        preferred_element_type=jnp.float32,
    )
    return mixed.astype(jnp.bfloat16)


def solution(mesh):
    in_specs = (
        P(("dp", "expert"), None),
        P(),
        P(),
        P("expert", None, "dp"),
        P("expert", None, "dp"),
        P("expert", "dp", None),
    )
    out_specs = P(("dp", "expert"), None)
    return jax.shard_map(shards, mesh=mesh, in_specs=in_specs, out_specs=out_specs, check_vma=False)
```

```python
import jax
import jax.numpy as jnp
from jax import lax
from jax.sharding import PartitionSpec as P

CHUNKS = 4


def slot_tables(chosen, tok_count):
    owners = chosen // tok_count
    capacity = chosen.shape[1]
    same = owners[:, :, None] == owners[:, None, :]
    earlier = (
        jnp.arange(capacity, dtype=jnp.int32)[None, :]
        < jnp.arange(capacity, dtype=jnp.int32)[:, None]
    )
    ranks = jnp.sum((same & earlier[None]).astype(jnp.int32), axis=2)
    return (owners, ranks)


def shards(tokens, chosen, combine_fixed, w_gate, w_up, w_down):
    dp_count = lax.axis_size("dp")
    ex_count = lax.axis_size("expert")
    worker_ordinal = dp_count * ex_count
    tok_count, model_width = tokens.shape
    expert_total, capacity = chosen.shape
    slot_count = min(tok_count, max(4, 2 * capacity // worker_ordinal))
    my_index = lax.axis_index("dp") * ex_count + lax.axis_index("expert")
    owners, ranks = slot_tables(chosen, tok_count)
    local_idx = chosen - owners * tok_count
    is_mine = owners == my_index
    matches = is_mine[:, :, None] & (
        ranks[:, :, None] == jnp.arange(slot_count, dtype=jnp.int32)[None, None, :]
    )
    match_int = matches.astype(jnp.int32)
    source_idx = jnp.sum(match_int * local_idx[:, :, None], axis=1)
    present = jnp.sum(match_int, axis=1)
    scaled = combine_fixed.astype(jnp.float32) / 65536.0
    weights = jnp.sum(matches.astype(jnp.float32) * scaled[:, :, None], axis=1)
    send_rows = jnp.take(tokens, source_idx.reshape(-1), axis=0)
    send_rows = jnp.where(present.reshape(-1, 1) > 0, send_rows, jnp.zeros_like(send_rows))
    placed = (jnp.arange(tok_count, dtype=jnp.int32)[:, None] == source_idx.reshape(1, -1)) & (
        present.reshape(1, -1) > 0
    )
    mixing = jnp.where(placed, weights.reshape(1, -1), 0.0)
    width = model_width // CHUNKS
    gate_act = None
    up_act = None
    for c in range(CHUNKS):
        cols = slice(c * width, (c + 1) * width)
        row_in = lax.all_to_all(send_rows[:, cols], "expert", split_axis=0, concat_axis=0, tiled=True)
        picked = lax.all_gather(row_in, "dp", axis=0, tiled=True)
        g = jnp.dot(picked, w_gate[0, cols], preferred_element_type=jnp.float32)
        u = jnp.dot(picked, w_up[0, cols], preferred_element_type=jnp.float32)
        gate_act = g if gate_act is None else gate_act + g
        up_act = u if up_act is None else up_act + u
    hidden = (jax.nn.silu(gate_act) * up_act).astype(jnp.bfloat16)
    pieces = []
    for c in range(CHUNKS):
        cols = slice(c * width, (c + 1) * width)
        result = jnp.dot(hidden, w_down[0, :, cols], preferred_element_type=jnp.float32).astype(jnp.bfloat16)
        summed = lax.psum_scatter(result, "dp", scatter_dimension=0, tiled=True)
        returned = lax.all_to_all(summed, "expert", split_axis=0, concat_axis=0, tiled=True)
        pieces.append(
            jnp.dot(
                mixing,
                returned.astype(jnp.float32),
                precision=lax.Precision.HIGHEST,
                preferred_element_type=jnp.float32,
            )
        )
    mixed = jnp.concatenate(pieces, axis=1)
    return mixed.astype(jnp.bfloat16)


def solution(mesh):
    in_specs = (
        P(("dp", "expert"), None),
        P(),
        P(),
        P("expert", None, "dp"),
        P("expert", None, "dp"),
        P("expert", "dp", None),
    )
    out_specs = P(("dp", "expert"), None)
    return jax.shard_map(shards, mesh=mesh, in_specs=in_specs, out_specs=out_specs, check_vma=False)
```

```python
import jax
import jax.numpy as jnp
from jax import lax
from jax.sharding import PartitionSpec as P


def slot_tables(chosen, tok_count):
    owners = chosen // tok_count
    capacity = chosen.shape[1]
    same = owners[:, :, None] == owners[:, None, :]
    earlier = (
        jnp.arange(capacity, dtype=jnp.int32)[None, :]
        < jnp.arange(capacity, dtype=jnp.int32)[:, None]
    )
    ranks = jnp.sum((same & earlier[None]).astype(jnp.int32), axis=2)
    return (owners, ranks)


def shards(tokens, chosen, combine_fixed, w_gate, w_up, w_down):
    dp_count = lax.axis_size("dp")
    ex_count = lax.axis_size("expert")
    worker_ordinal = dp_count * ex_count
    tok_count, model_width = tokens.shape
    expert_total, capacity = chosen.shape
    slot_count = min(tok_count, max(4, 2 * capacity // worker_ordinal))
    my_index = lax.axis_index("dp") * ex_count + lax.axis_index("expert")
    owners, ranks = slot_tables(chosen, tok_count)
    local_idx = chosen - owners * tok_count
    is_mine = owners == my_index
    matches = is_mine[:, :, None] & (
        ranks[:, :, None] == jnp.arange(slot_count, dtype=jnp.int32)[None, None, :]
    )
    match_int = matches.astype(jnp.int32)
    source_idx = jnp.sum(match_int * local_idx[:, :, None], axis=1)
    present = jnp.sum(match_int, axis=1)
    scaled = combine_fixed.astype(jnp.float32) / 65536.0
    weights = jnp.sum(matches.astype(jnp.float32) * scaled[:, :, None], axis=1)
    send_rows = jnp.take(tokens, source_idx.reshape(-1), axis=0)
    send_rows = jnp.where(present.reshape(-1, 1) > 0, send_rows, jnp.zeros_like(send_rows))
    row_in = lax.all_to_all(send_rows, "expert", split_axis=0, concat_axis=0, tiled=True)
    picked = lax.all_gather(row_in, "dp", axis=0, tiled=True)
    gate_act = jnp.dot(picked, w_gate[0], preferred_element_type=jnp.float32)
    up_act = jnp.dot(picked, w_up[0], preferred_element_type=jnp.float32)
    hidden = (jax.nn.silu(gate_act) * up_act).astype(jnp.bfloat16)
    hidden = lax.optimization_barrier(hidden)
    result = jnp.dot(hidden, w_down[0], preferred_element_type=jnp.float32).astype(jnp.bfloat16)
    summed = lax.psum_scatter(result, "dp", scatter_dimension=0, tiled=True)
    returned = lax.all_to_all(summed, "expert", split_axis=0, concat_axis=0, tiled=True)
    placed = (jnp.arange(tok_count, dtype=jnp.int32)[:, None] == source_idx.reshape(1, -1)) & (
        present.reshape(1, -1) > 0
    )
    mixing = jnp.where(placed, weights.reshape(1, -1), 0.0)
    mix_hi = mixing.astype(jnp.bfloat16)
    mix_lo = (mixing - mix_hi.astype(jnp.float32)).astype(jnp.bfloat16)
    mixed = jnp.dot(mix_hi, returned, preferred_element_type=jnp.float32) + jnp.dot(
        mix_lo, returned, preferred_element_type=jnp.float32
    )
    return mixed.astype(jnp.bfloat16)


def solution(mesh):
    in_specs = (
        P(("dp", "expert"), None),
        P(),
        P(),
        P("expert", None, "dp"),
        P("expert", None, "dp"),
        P("expert", "dp", None),
    )
    out_specs = P(("dp", "expert"), None)
    return jax.shard_map(shards, mesh=mesh, in_specs=in_specs, out_specs=out_specs, check_vma=False)
```

```python
import jax
import jax.numpy as jnp
from jax import lax
from jax.sharding import PartitionSpec as P


def slot_tables(chosen, tok_count):
    owners = chosen // tok_count
    capacity = chosen.shape[1]
    same = owners[:, :, None] == owners[:, None, :]
    earlier = (
        jnp.arange(capacity, dtype=jnp.int32)[None, :]
        < jnp.arange(capacity, dtype=jnp.int32)[:, None]
    )
    ranks = jnp.sum((same & earlier[None]).astype(jnp.int32), axis=2)
    return (owners, ranks)


def dp_pairs(dp_count, shift):
    ny = dp_count // 2
    return [(y * 2 + c, ((y + shift) % ny) * 2 + c) for y in range(ny) for c in range(2)]


def sib_pairs(dp_count):
    return [(y * 2 + c, y * 2 + 1 - c) for y in range(dp_count // 2) for c in range(2)]


def gather_dp(x, dp_count):
    half = x.shape[1] // 2
    up = lax.ppermute(x, "dp", dp_pairs(dp_count, 1))
    dn = lax.ppermute(x, "dp", dp_pairs(dp_count, -1))
    sib = lax.ppermute(x, "dp", sib_pairs(dp_count))
    far_a = lax.ppermute(up[:, :half], "dp", dp_pairs(dp_count, 1))
    far_b = lax.ppermute(dn[:, half:], "dp", dp_pairs(dp_count, -1))
    far = jnp.concatenate([far_a, far_b], axis=1)
    s_up = lax.ppermute(up, "dp", sib_pairs(dp_count))
    s_dn = lax.ppermute(dn, "dp", sib_pairs(dp_count))
    s_far = lax.ppermute(far, "dp", sib_pairs(dp_count))
    return jnp.concatenate([x, sib, up, s_up, dn, s_dn, far, s_far], axis=0)


def scatter_dp(p, dp_count):
    rows = p.shape[0] // 8
    half = p.shape[1] // 2
    f32 = jnp.float32
    b = [p[i * rows:(i + 1) * rows] for i in range(8)]
    got = lax.ppermute(jnp.concatenate([b[1], b[3], b[5], b[7]], axis=0), "dp", sib_pairs(dp_count))
    g = [got[i * rows:(i + 1) * rows].astype(f32) for i in range(4)]
    q_self = b[0].astype(f32) + g[0]
    q_up = b[2].astype(f32) + g[1]
    q_dn = b[4].astype(f32) + g[2]
    q_far = (b[6].astype(f32) + g[3]).astype(jnp.bfloat16)
    r_a = lax.ppermute(q_far[:, :half], "dp", dp_pairs(dp_count, 1)).astype(f32)
    r_b = lax.ppermute(q_far[:, half:], "dp", dp_pairs(dp_count, -1)).astype(f32)
    s_a = jnp.concatenate([q_dn[:, :half] + r_a, q_dn[:, half:]], axis=1).astype(jnp.bfloat16)
    s_b = jnp.concatenate([q_up[:, :half], q_up[:, half:] + r_b], axis=1).astype(jnp.bfloat16)
    a_a = lax.ppermute(s_a, "dp", dp_pairs(dp_count, 1)).astype(f32)
    a_b = lax.ppermute(s_b, "dp", dp_pairs(dp_count, -1)).astype(f32)
    return (q_self + a_a + a_b).astype(jnp.bfloat16)


def shards(tokens, chosen, combine_fixed, w_gate, w_up, w_down):
    dp_count = lax.axis_size("dp")
    ex_count = lax.axis_size("expert")
    worker_ordinal = dp_count * ex_count
    tok_count, model_width = tokens.shape
    expert_total, capacity = chosen.shape
    slot_count = min(tok_count, max(4, 2 * capacity // worker_ordinal))
    my_index = lax.axis_index("dp") * ex_count + lax.axis_index("expert")
    owners, ranks = slot_tables(chosen, tok_count)
    local_idx = chosen - owners * tok_count
    is_mine = owners == my_index
    matches = is_mine[:, :, None] & (
        ranks[:, :, None] == jnp.arange(slot_count, dtype=jnp.int32)[None, None, :]
    )
    match_int = matches.astype(jnp.int32)
    source_idx = jnp.sum(match_int * local_idx[:, :, None], axis=1)
    present = jnp.sum(match_int, axis=1)
    scaled = combine_fixed.astype(jnp.float32) / 65536.0
    weights = jnp.sum(matches.astype(jnp.float32) * scaled[:, :, None], axis=1)
    send_rows = jnp.take(tokens, source_idx.reshape(-1), axis=0)
    send_rows = jnp.where(present.reshape(-1, 1) > 0, send_rows, jnp.zeros_like(send_rows))
    row_in = lax.all_to_all(send_rows, "expert", split_axis=0, concat_axis=0, tiled=True)
    picked = gather_dp(row_in, dp_count)
    gate_act = jnp.dot(picked, w_gate[0], preferred_element_type=jnp.float32)
    up_act = jnp.dot(picked, w_up[0], preferred_element_type=jnp.float32)
    hidden = (jax.nn.silu(gate_act) * up_act).astype(jnp.bfloat16)
    hidden = lax.optimization_barrier(hidden)
    result = jnp.dot(hidden, w_down[0], preferred_element_type=jnp.float32).astype(jnp.bfloat16)
    summed = scatter_dp(result, dp_count)
    returned = lax.all_to_all(summed, "expert", split_axis=0, concat_axis=0, tiled=True)
    placed = (jnp.arange(tok_count, dtype=jnp.int32)[:, None] == source_idx.reshape(1, -1)) & (
        present.reshape(1, -1) > 0
    )
    mixing = jnp.where(placed, weights.reshape(1, -1), 0.0)
    mix_hi = mixing.astype(jnp.bfloat16)
    mix_lo = (mixing - mix_hi.astype(jnp.float32)).astype(jnp.bfloat16)
    mixed = jnp.dot(mix_hi, returned, preferred_element_type=jnp.float32) + jnp.dot(
        mix_lo, returned, preferred_element_type=jnp.float32
    )
    return mixed.astype(jnp.bfloat16)


def solution(mesh):
    in_specs = (
        P(("dp", "expert"), None),
        P(),
        P(),
        P("expert", None, "dp"),
        P("expert", None, "dp"),
        P("expert", "dp", None),
    )
    out_specs = P(("dp", "expert"), None)
    return jax.shard_map(shards, mesh=mesh, in_specs=in_specs, out_specs=out_specs, check_vma=False)
```

```python
import jax
import jax.numpy as jnp
from jax import lax
from jax.sharding import PartitionSpec as P


def slot_tables(chosen, tok_count):
    owners = chosen // tok_count
    capacity = chosen.shape[1]
    same = owners[:, :, None] == owners[:, None, :]
    earlier = (
        jnp.arange(capacity, dtype=jnp.int32)[None, :]
        < jnp.arange(capacity, dtype=jnp.int32)[:, None]
    )
    ranks = jnp.sum((same & earlier[None]).astype(jnp.int32), axis=2)
    return (owners, ranks)


def dp_pairs(dp_count, shift):
    ny = dp_count // 2
    return [(y * 2 + c, ((y + shift) % ny) * 2 + c) for y in range(ny) for c in range(2)]


def sib_pairs(dp_count):
    return [(y * 2 + c, y * 2 + 1 - c) for y in range(dp_count // 2) for c in range(2)]


def gather_dp(x, dp_count):
    half = x.shape[1] // 2
    up = lax.ppermute(x, "dp", dp_pairs(dp_count, 1))
    dn = lax.ppermute(x, "dp", dp_pairs(dp_count, -1))
    sib = lax.ppermute(x, "dp", sib_pairs(dp_count))
    far_a = lax.ppermute(up[:, :half], "dp", dp_pairs(dp_count, 1))
    far_b = lax.ppermute(dn[:, half:], "dp", dp_pairs(dp_count, -1))
    far = jnp.concatenate([far_a, far_b], axis=1)
    s_up = lax.ppermute(up, "dp", sib_pairs(dp_count))
    s_dn = lax.ppermute(dn, "dp", sib_pairs(dp_count))
    s_far = lax.ppermute(far, "dp", sib_pairs(dp_count))
    return jnp.concatenate([x, sib, up, s_up, dn, s_dn, far, s_far], axis=0)


def scatter_dp(p, dp_count):
    rows = p.shape[0] // 8
    half = p.shape[1] // 2
    f32 = jnp.float32
    b = [p[i * rows:(i + 1) * rows] for i in range(8)]
    got = lax.ppermute(jnp.concatenate([b[1], b[3], b[5], b[7]], axis=0), "dp", sib_pairs(dp_count))
    g = [got[i * rows:(i + 1) * rows].astype(f32) for i in range(4)]
    q_self = b[0].astype(f32) + g[0]
    q_up = b[2].astype(f32) + g[1]
    q_dn = b[4].astype(f32) + g[2]
    q_far = (b[6].astype(f32) + g[3]).astype(jnp.bfloat16)
    r_a = lax.ppermute(q_far[:, :half], "dp", dp_pairs(dp_count, 1)).astype(f32)
    r_b = lax.ppermute(q_far[:, half:], "dp", dp_pairs(dp_count, -1)).astype(f32)
    s_a = jnp.concatenate([q_dn[:, :half] + r_a, q_dn[:, half:]], axis=1).astype(jnp.bfloat16)
    s_b = jnp.concatenate([q_up[:, :half], q_up[:, half:] + r_b], axis=1).astype(jnp.bfloat16)
    a_a = lax.ppermute(s_a, "dp", dp_pairs(dp_count, 1)).astype(f32)
    a_b = lax.ppermute(s_b, "dp", dp_pairs(dp_count, -1)).astype(f32)
    return (q_self + a_a + a_b).astype(jnp.bfloat16)


def shards(tokens, chosen, combine_fixed, w_gate, w_up, w_down):
    dp_count = lax.axis_size("dp")
    ex_count = lax.axis_size("expert")
    worker_ordinal = dp_count * ex_count
    tok_count, model_width = tokens.shape
    expert_total, capacity = chosen.shape
    slot_count = min(tok_count, max(4, 2 * capacity // worker_ordinal))
    my_index = lax.axis_index("dp") * ex_count + lax.axis_index("expert")
    owners, ranks = slot_tables(chosen, tok_count)
    local_idx = chosen - owners * tok_count
    my_expert = lax.axis_index("expert")
    rel = (my_expert + jnp.arange(expert_total, dtype=jnp.int32)) % ex_count
    owners = jnp.take(owners, rel, axis=0)
    ranks = jnp.take(ranks, rel, axis=0)
    local_idx = jnp.take(local_idx, rel, axis=0)
    combine_rel = jnp.take(combine_fixed, rel, axis=0)
    is_mine = owners == my_index
    matches = is_mine[:, :, None] & (
        ranks[:, :, None] == jnp.arange(slot_count, dtype=jnp.int32)[None, None, :]
    )
    match_int = matches.astype(jnp.int32)
    source_idx = jnp.sum(match_int * local_idx[:, :, None], axis=1)
    present = jnp.sum(match_int, axis=1)
    scaled = combine_rel.astype(jnp.float32) / 65536.0
    weights = jnp.sum(matches.astype(jnp.float32) * scaled[:, :, None], axis=1)
    send_rows = jnp.take(tokens, source_idx.reshape(-1), axis=0)
    send_rows = jnp.where(present.reshape(-1, 1) > 0, send_rows, jnp.zeros_like(send_rows))
    blocks = [send_rows[:slot_count]]
    for k in range(1, ex_count):
        pairs = [(j, (j + k) % ex_count) for j in range(ex_count)]
        blocks.append(lax.ppermute(send_rows[k * slot_count:(k + 1) * slot_count], "expert", pairs))
    row_in = jnp.concatenate(blocks, axis=0)
    picked = gather_dp(row_in, dp_count)
    gate_act = jnp.dot(picked, w_gate[0], preferred_element_type=jnp.float32)
    up_act = jnp.dot(picked, w_up[0], preferred_element_type=jnp.float32)
    hidden = (jax.nn.silu(gate_act) * up_act).astype(jnp.bfloat16)
    hidden = lax.optimization_barrier(hidden)
    result = jnp.dot(hidden, w_down[0], preferred_element_type=jnp.float32).astype(jnp.bfloat16)
    summed = scatter_dp(result, dp_count)
    back = [summed[:slot_count]]
    for k in range(1, ex_count):
        pairs = [(i, (i - k) % ex_count) for i in range(ex_count)]
        back.append(lax.ppermute(summed[k * slot_count:(k + 1) * slot_count], "expert", pairs))
    returned = jnp.concatenate(back, axis=0)
    placed = (jnp.arange(tok_count, dtype=jnp.int32)[:, None] == source_idx.reshape(1, -1)) & (
        present.reshape(1, -1) > 0
    )
    mixing = jnp.where(placed, weights.reshape(1, -1), 0.0)
    mix_hi = mixing.astype(jnp.bfloat16)
    mix_lo = (mixing - mix_hi.astype(jnp.float32)).astype(jnp.bfloat16)
    mixed = jnp.dot(mix_hi, returned, preferred_element_type=jnp.float32) + jnp.dot(
        mix_lo, returned, preferred_element_type=jnp.float32
    )
    return mixed.astype(jnp.bfloat16)


def solution(mesh):
    in_specs = (
        P(("dp", "expert"), None),
        P(),
        P(),
        P("expert", None, "dp"),
        P("expert", None, "dp"),
        P("expert", "dp", None),
    )
    out_specs = P(("dp", "expert"), None)
    return jax.shard_map(shards, mesh=mesh, in_specs=in_specs, out_specs=out_specs, check_vma=False)
```

```python
import jax
import jax.numpy as jnp
from jax import lax
from jax.sharding import PartitionSpec as P


def slot_tables(chosen, tok_count, my_index):
    owners = chosen // tok_count
    capacity = chosen.shape[1]
    is_mine = owners == my_index
    earlier = (
        jnp.arange(capacity, dtype=jnp.int32)[:, None]
        < jnp.arange(capacity, dtype=jnp.int32)[None, :]
    ).astype(jnp.bfloat16)
    ranks = jnp.dot(is_mine.astype(jnp.bfloat16), earlier, preferred_element_type=jnp.float32)
    return (owners, is_mine, ranks.astype(jnp.int32))

def dp_pairs(dp_count, shift):
    ny = dp_count // 2
    return [(y * 2 + c, ((y + shift) % ny) * 2 + c) for y in range(ny) for c in range(2)]


def sib_pairs(dp_count):
    return [(y * 2 + c, y * 2 + 1 - c) for y in range(dp_count // 2) for c in range(2)]


def gather_dp(x, dp_count):
    half = x.shape[1] // 2
    up = lax.ppermute(x, "dp", dp_pairs(dp_count, 1))
    dn = lax.ppermute(x, "dp", dp_pairs(dp_count, -1))
    sib = lax.ppermute(x, "dp", sib_pairs(dp_count))
    far_a = lax.ppermute(up[:, :half], "dp", dp_pairs(dp_count, 1))
    far_b = lax.ppermute(dn[:, half:], "dp", dp_pairs(dp_count, -1))
    far = jnp.concatenate([far_a, far_b], axis=1)
    s_up = lax.ppermute(up, "dp", sib_pairs(dp_count))
    s_dn = lax.ppermute(dn, "dp", sib_pairs(dp_count))
    s_far = lax.ppermute(far, "dp", sib_pairs(dp_count))
    return jnp.concatenate([x, sib, up, s_up, dn, s_dn, far, s_far], axis=0)


def scatter_dp(p, dp_count):
    rows = p.shape[0] // 8
    half = p.shape[1] // 2
    f32 = jnp.float32
    b = [p[i * rows:(i + 1) * rows] for i in range(8)]
    got_far = lax.ppermute(b[7], "dp", sib_pairs(dp_count))
    got = lax.ppermute(jnp.concatenate([b[1], b[3], b[5]], axis=0), "dp", sib_pairs(dp_count))
    g = [got[i * rows:(i + 1) * rows].astype(f32) for i in range(3)] + [got_far.astype(f32)]
    q_self = b[0].astype(f32) + g[0]
    q_up = b[2].astype(f32) + g[1]
    q_dn = b[4].astype(f32) + g[2]
    q_far = (b[6].astype(f32) + g[3]).astype(jnp.bfloat16)
    r_a = lax.ppermute(q_far[:, :half], "dp", dp_pairs(dp_count, 1)).astype(f32)
    r_b = lax.ppermute(q_far[:, half:], "dp", dp_pairs(dp_count, -1)).astype(f32)
    s_a = jnp.concatenate([q_dn[:, :half] + r_a, q_dn[:, half:]], axis=1).astype(jnp.bfloat16)
    s_b = jnp.concatenate([q_up[:, :half], q_up[:, half:] + r_b], axis=1).astype(jnp.bfloat16)
    a_a = lax.ppermute(s_a, "dp", dp_pairs(dp_count, 1)).astype(f32)
    a_b = lax.ppermute(s_b, "dp", dp_pairs(dp_count, -1)).astype(f32)
    return (q_self + a_a + a_b).astype(jnp.bfloat16)


def shards(tokens, chosen, combine_fixed, w_gate, w_up, w_down):
    dp_count = lax.axis_size("dp")
    ex_count = lax.axis_size("expert")
    worker_ordinal = dp_count * ex_count
    tok_count, model_width = tokens.shape
    expert_total, capacity = chosen.shape
    slot_count = min(tok_count, max(4, 2 * capacity // worker_ordinal))
    my_index = lax.axis_index("dp") * ex_count + lax.axis_index("expert")
    owners, is_mine, ranks = slot_tables(chosen, tok_count, my_index)
    local_idx = chosen - owners * tok_count
    matches = is_mine[:, :, None] & (
        ranks[:, :, None] == jnp.arange(slot_count, dtype=jnp.int32)[None, None, :]
    )
    match_int = matches.astype(jnp.int32)
    source_idx = jnp.sum(match_int * local_idx[:, :, None], axis=1)
    present = jnp.sum(match_int, axis=1)
    scaled = combine_fixed.astype(jnp.float32) / 65536.0
    weights = jnp.sum(matches.astype(jnp.float32) * scaled[:, :, None], axis=1)
    send_rows = jnp.take(tokens, source_idx.reshape(-1), axis=0)
    send_rows = jnp.where(present.reshape(-1, 1) > 0, send_rows, jnp.zeros_like(send_rows))
    row_in = lax.all_to_all(send_rows, "expert", split_axis=0, concat_axis=0, tiled=True)
    picked = gather_dp(row_in, dp_count)
    gate_act = jnp.dot(picked, w_gate[0], preferred_element_type=jnp.float32)
    up_act = jnp.dot(picked, w_up[0], preferred_element_type=jnp.float32)
    hidden = (jax.nn.silu(gate_act) * up_act).astype(jnp.bfloat16)
    hidden = lax.optimization_barrier(hidden)
    result = jnp.dot(hidden, w_down[0], preferred_element_type=jnp.float32).astype(jnp.bfloat16)
    summed = scatter_dp(result, dp_count)
    returned = lax.all_to_all(summed, "expert", split_axis=0, concat_axis=0, tiled=True)
    placed = (jnp.arange(tok_count, dtype=jnp.int32)[:, None] == source_idx.reshape(1, -1)) & (
        present.reshape(1, -1) > 0
    )
    mixing = jnp.where(placed, weights.reshape(1, -1), 0.0)
    mix_hi = mixing.astype(jnp.bfloat16)
    mix_lo = (mixing - mix_hi.astype(jnp.float32)).astype(jnp.bfloat16)
    mixed = jnp.dot(mix_hi, returned, preferred_element_type=jnp.float32) + jnp.dot(
        mix_lo, returned, preferred_element_type=jnp.float32
    )
    return mixed.astype(jnp.bfloat16)


def solution(mesh):
    in_specs = (
        P(("dp", "expert"), None),
        P(),
        P(),
        P("expert", None, "dp"),
        P("expert", None, "dp"),
        P("expert", "dp", None),
    )
    out_specs = P(("dp", "expert"), None)
    return jax.shard_map(shards, mesh=mesh, in_specs=in_specs, out_specs=out_specs, check_vma=False)
```

```python
import jax
import jax.numpy as jnp
from jax import lax
from jax.sharding import PartitionSpec as P


def slot_tables(chosen, tok_count, my_index):
    owners = chosen // tok_count
    capacity = chosen.shape[1]
    is_mine = owners == my_index
    earlier = (
        jnp.arange(capacity, dtype=jnp.int32)[:, None]
        < jnp.arange(capacity, dtype=jnp.int32)[None, :]
    ).astype(jnp.bfloat16)
    ranks = jnp.dot(is_mine.astype(jnp.bfloat16), earlier, preferred_element_type=jnp.float32)
    return (owners, is_mine, ranks.astype(jnp.int32))

def dp_pairs(dp_count, shift):
    ny = dp_count // 2
    return [(y * 2 + c, ((y + shift) % ny) * 2 + c) for y in range(ny) for c in range(2)]


def sib_pairs(dp_count):
    return [(y * 2 + c, y * 2 + 1 - c) for y in range(dp_count // 2) for c in range(2)]


def gather_dp(x, dp_count):
    half = x.shape[1] // 2
    up = lax.ppermute(x, "dp", dp_pairs(dp_count, 1))
    dn = lax.ppermute(x, "dp", dp_pairs(dp_count, -1))
    sib = lax.ppermute(x, "dp", sib_pairs(dp_count))
    far_a = lax.ppermute(up[:, :half], "dp", dp_pairs(dp_count, 1))
    far_b = lax.ppermute(dn[:, half:], "dp", dp_pairs(dp_count, -1))
    far = jnp.concatenate([far_a, far_b], axis=1)
    s_up = lax.ppermute(up, "dp", sib_pairs(dp_count))
    s_dn = lax.ppermute(dn, "dp", sib_pairs(dp_count))
    s_far = lax.ppermute(far, "dp", sib_pairs(dp_count))
    return jnp.concatenate([x, sib, up, s_up, dn, s_dn, far, s_far], axis=0)


def scatter_dp(p, dp_count):
    rows = p.shape[0] // 8
    half = p.shape[1] // 2
    f32 = jnp.float32
    b = [p[i * rows:(i + 1) * rows] for i in range(8)]
    got_far = lax.ppermute(b[7], "dp", sib_pairs(dp_count))
    got = lax.ppermute(jnp.concatenate([b[1], b[3], b[5]], axis=0), "dp", sib_pairs(dp_count))
    g = [got[i * rows:(i + 1) * rows].astype(f32) for i in range(3)] + [got_far.astype(f32)]
    q_self = b[0].astype(f32) + g[0]
    q_up = b[2].astype(f32) + g[1]
    q_dn = b[4].astype(f32) + g[2]
    q_far = (b[6].astype(f32) + g[3]).astype(jnp.bfloat16)
    r_a = lax.ppermute(q_far[:, :half], "dp", dp_pairs(dp_count, 1)).astype(f32)
    r_b = lax.ppermute(q_far[:, half:], "dp", dp_pairs(dp_count, -1)).astype(f32)
    s_a = jnp.concatenate([q_dn[:, :half] + r_a, q_dn[:, half:]], axis=1).astype(jnp.bfloat16)
    s_b = jnp.concatenate([q_up[:, :half], q_up[:, half:] + r_b], axis=1).astype(jnp.bfloat16)
    a_a = lax.ppermute(s_a, "dp", dp_pairs(dp_count, 1)).astype(f32)
    a_b = lax.ppermute(s_b, "dp", dp_pairs(dp_count, -1)).astype(f32)
    return (q_self + a_a + a_b).astype(jnp.bfloat16)


def shards(tokens, chosen, combine_fixed, w_gate, w_up, w_down):
    dp_count = lax.axis_size("dp")
    ex_count = lax.axis_size("expert")
    worker_ordinal = dp_count * ex_count
    tok_count, model_width = tokens.shape
    expert_total, capacity = chosen.shape
    slot_count = min(tok_count, max(4, 2 * capacity // worker_ordinal))
    my_index = lax.axis_index("dp") * ex_count + lax.axis_index("expert")
    owners, is_mine, ranks = slot_tables(chosen, tok_count, my_index)
    local_idx = chosen - owners * tok_count
    matches = is_mine[:, :, None] & (
        ranks[:, :, None] == jnp.arange(slot_count, dtype=jnp.int32)[None, None, :]
    )
    match_int = matches.astype(jnp.int32)
    source_idx = jnp.sum(match_int * local_idx[:, :, None], axis=1)
    present = jnp.sum(match_int, axis=1)
    scaled = combine_fixed.astype(jnp.float32) / 65536.0
    weights = jnp.sum(matches.astype(jnp.float32) * scaled[:, :, None], axis=1)
    send_rows = jnp.take(tokens, source_idx.reshape(-1), axis=0)
    send_rows = jnp.where(present.reshape(-1, 1) > 0, send_rows, jnp.zeros_like(send_rows))
    halves = 2
    width = model_width // halves
    gate_act = None
    up_act = None
    for c in range(halves):
        cols = slice(c * width, (c + 1) * width)
        row_in = lax.all_to_all(send_rows[:, cols], "expert", split_axis=0, concat_axis=0, tiled=True)
        picked = gather_dp(row_in, dp_count)
        g = jnp.dot(picked, w_gate[0, cols], preferred_element_type=jnp.float32)
        u = jnp.dot(picked, w_up[0, cols], preferred_element_type=jnp.float32)
        gate_act = g if gate_act is None else gate_act + g
        up_act = u if up_act is None else up_act + u
    hidden = (jax.nn.silu(gate_act) * up_act).astype(jnp.bfloat16)
    hidden = lax.optimization_barrier(hidden)
    back = []
    for c in range(halves):
        cols = slice(c * width, (c + 1) * width)
        result = jnp.dot(hidden, w_down[0, :, cols], preferred_element_type=jnp.float32).astype(jnp.bfloat16)
        summed = scatter_dp(result, dp_count)
        back.append(lax.all_to_all(summed, "expert", split_axis=0, concat_axis=0, tiled=True))
    returned = jnp.concatenate(back, axis=1)
    placed = (jnp.arange(tok_count, dtype=jnp.int32)[:, None] == source_idx.reshape(1, -1)) & (
        present.reshape(1, -1) > 0
    )
    mixing = jnp.where(placed, weights.reshape(1, -1), 0.0)
    mix_hi = mixing.astype(jnp.bfloat16)
    mix_lo = (mixing - mix_hi.astype(jnp.float32)).astype(jnp.bfloat16)
    mixed = jnp.dot(mix_hi, returned, preferred_element_type=jnp.float32) + jnp.dot(
        mix_lo, returned, preferred_element_type=jnp.float32
    )
    return mixed.astype(jnp.bfloat16)


def solution(mesh):
    in_specs = (
        P(("dp", "expert"), None),
        P(),
        P(),
        P("expert", None, "dp"),
        P("expert", None, "dp"),
        P("expert", "dp", None),
    )
    out_specs = P(("dp", "expert"), None)
    return jax.shard_map(shards, mesh=mesh, in_specs=in_specs, out_specs=out_specs, check_vma=False)
```

```python
import jax
import jax.numpy as jnp
from jax import lax
from jax.sharding import PartitionSpec as P

COMPACT_ROWS = 56


def slot_tables(chosen, tok_count, my_index):
    owners = chosen // tok_count
    capacity = chosen.shape[1]
    is_mine = owners == my_index
    earlier = (
        jnp.arange(capacity, dtype=jnp.int32)[:, None]
        < jnp.arange(capacity, dtype=jnp.int32)[None, :]
    ).astype(jnp.bfloat16)
    ranks = jnp.dot(is_mine.astype(jnp.bfloat16), earlier, preferred_element_type=jnp.float32)
    return (owners, is_mine, ranks.astype(jnp.int32))

def dp_pairs(dp_count, shift):
    ny = dp_count // 2
    return [(y * 2 + c, ((y + shift) % ny) * 2 + c) for y in range(ny) for c in range(2)]


def sib_pairs(dp_count):
    return [(y * 2 + c, y * 2 + 1 - c) for y in range(dp_count // 2) for c in range(2)]


def gather_dp(x, dp_count):
    half = x.shape[1] // 2
    up = lax.ppermute(x, "dp", dp_pairs(dp_count, 1))
    dn = lax.ppermute(x, "dp", dp_pairs(dp_count, -1))
    sib = lax.ppermute(x, "dp", sib_pairs(dp_count))
    far_a = lax.ppermute(up[:, :half], "dp", dp_pairs(dp_count, 1))
    far_b = lax.ppermute(dn[:, half:], "dp", dp_pairs(dp_count, -1))
    far = jnp.concatenate([far_a, far_b], axis=1)
    s_up = lax.ppermute(up, "dp", sib_pairs(dp_count))
    s_dn = lax.ppermute(dn, "dp", sib_pairs(dp_count))
    s_far = lax.ppermute(far, "dp", sib_pairs(dp_count))
    return jnp.concatenate([x, sib, up, s_up, dn, s_dn, far, s_far], axis=0)


def scatter_dp(p, dp_count):
    rows = p.shape[0] // 8
    half = p.shape[1] // 2
    f32 = jnp.float32
    b = [p[i * rows:(i + 1) * rows] for i in range(8)]
    got_far = lax.ppermute(b[7], "dp", sib_pairs(dp_count))
    got = lax.ppermute(jnp.concatenate([b[1], b[3], b[5]], axis=0), "dp", sib_pairs(dp_count))
    g = [got[i * rows:(i + 1) * rows].astype(f32) for i in range(3)] + [got_far.astype(f32)]
    q_self = b[0].astype(f32) + g[0]
    q_up = b[2].astype(f32) + g[1]
    q_dn = b[4].astype(f32) + g[2]
    q_far = (b[6].astype(f32) + g[3]).astype(jnp.bfloat16)
    r_a = lax.ppermute(q_far[:, :half], "dp", dp_pairs(dp_count, 1)).astype(f32)
    r_b = lax.ppermute(q_far[:, half:], "dp", dp_pairs(dp_count, -1)).astype(f32)
    s_a = jnp.concatenate([q_dn[:, :half] + r_a, q_dn[:, half:]], axis=1).astype(jnp.bfloat16)
    s_b = jnp.concatenate([q_up[:, :half], q_up[:, half:] + r_b], axis=1).astype(jnp.bfloat16)
    a_a = lax.ppermute(s_a, "dp", dp_pairs(dp_count, 1)).astype(f32)
    a_b = lax.ppermute(s_b, "dp", dp_pairs(dp_count, -1)).astype(f32)
    return (q_self + a_a + a_b).astype(jnp.bfloat16)


def shards(tokens, chosen, combine_fixed, w_gate, w_up, w_down):
    dp_count = lax.axis_size("dp")
    ex_count = lax.axis_size("expert")
    worker_ordinal = dp_count * ex_count
    tok_count, model_width = tokens.shape
    expert_total, capacity = chosen.shape
    slot_count = min(tok_count, max(4, 2 * capacity // worker_ordinal))
    my_index = lax.axis_index("dp") * ex_count + lax.axis_index("expert")
    my_expert_idx = lax.axis_index("expert")
    owners, is_mine, ranks = slot_tables(chosen, tok_count, my_index)
    local_idx = chosen - owners * tok_count
    matches = is_mine[:, :, None] & (
        ranks[:, :, None] == jnp.arange(slot_count, dtype=jnp.int32)[None, None, :]
    )
    match_int = matches.astype(jnp.int32)
    source_idx = jnp.sum(match_int * local_idx[:, :, None], axis=1)
    present = jnp.sum(match_int, axis=1)
    scaled = combine_fixed.astype(jnp.float32) / 65536.0
    weights = jnp.sum(matches.astype(jnp.float32) * scaled[:, :, None], axis=1)
    send_rows = jnp.take(tokens, source_idx.reshape(-1), axis=0)
    send_rows = jnp.where(present.reshape(-1, 1) > 0, send_rows, jnp.zeros_like(send_rows))
    row_in = lax.all_to_all(send_rows, "expert", split_axis=0, concat_axis=0, tiled=True)
    def expert_rows(rows, w_g, w_u, w_d):
        picked = gather_dp(rows, dp_count)
        gate_act = jnp.dot(picked, w_g, preferred_element_type=jnp.float32)
        up_act = jnp.dot(picked, w_u, preferred_element_type=jnp.float32)
        hidden = (jax.nn.silu(gate_act) * up_act).astype(jnp.bfloat16)
        hidden = lax.optimization_barrier(hidden)
        result = jnp.dot(hidden, w_d, preferred_element_type=jnp.float32).astype(jnp.bfloat16)
        return scatter_dp(result, dp_count)

    dp_rows = owners // ex_count
    my_dp = lax.axis_index("dp")
    counts = jnp.sum(
        (dp_rows[:, :, None] == jnp.arange(dp_count, dtype=jnp.int32)[None, None, :]).astype(jnp.int32),
        axis=1,
    )
    compact = min(ex_count * slot_count, COMPACT_ROWS)
    row_owners = lax.dynamic_index_in_dim(owners, my_expert_idx, 0, keepdims=False)
    same_owner = row_owners[:, None] == row_owners[None, :]
    tri = (
        jnp.arange(capacity, dtype=jnp.int32)[:, None]
        < jnp.arange(capacity, dtype=jnp.int32)[None, :]
    )
    row_ranks = jnp.sum((same_owner & tri).astype(jnp.int32), axis=0)
    in_group = (row_owners // ex_count) == my_dp
    group_pos = jnp.sum((in_group[:, None] & tri).astype(jnp.int32), axis=0)
    slot_of = (row_owners % ex_count) * slot_count + row_ranks
    pick_q = in_group[None, :] & (group_pos[None, :] == jnp.arange(compact, dtype=jnp.int32)[:, None])
    comp_src = jnp.sum(pick_q.astype(jnp.int32) * slot_of[None, :], axis=1)
    comp_ok = jnp.sum(pick_q.astype(jnp.int32), axis=1) > 0
    pick_s = in_group[None, :] & (
        slot_of[None, :] == jnp.arange(ex_count * slot_count, dtype=jnp.int32)[:, None]
    )
    back_src = jnp.sum(pick_s.astype(jnp.int32) * group_pos[None, :], axis=1)
    back_ok = jnp.sum(pick_s.astype(jnp.int32), axis=1) > 0

    def short_path(rows, w_g, w_u, w_d):
        packed = jnp.take(rows, comp_src, axis=0)
        packed = jnp.where(comp_ok[:, None], packed, jnp.zeros_like(packed))
        out = expert_rows(packed, w_g, w_u, w_d)
        spread = jnp.take(out, back_src, axis=0)
        return jnp.where(back_ok[:, None], spread, jnp.zeros_like(spread))

    summed = lax.cond(
        jnp.max(counts) <= compact, short_path, expert_rows, row_in, w_gate[0], w_up[0], w_down[0]
    )
    returned = lax.all_to_all(summed, "expert", split_axis=0, concat_axis=0, tiled=True)
    placed = (jnp.arange(tok_count, dtype=jnp.int32)[:, None] == source_idx.reshape(1, -1)) & (
        present.reshape(1, -1) > 0
    )
    mixing = jnp.where(placed, weights.reshape(1, -1), 0.0)
    mix_hi = mixing.astype(jnp.bfloat16)
    mix_lo = (mixing - mix_hi.astype(jnp.float32)).astype(jnp.bfloat16)
    mixed = jnp.dot(mix_hi, returned, preferred_element_type=jnp.float32) + jnp.dot(
        mix_lo, returned, preferred_element_type=jnp.float32
    )
    return mixed.astype(jnp.bfloat16)


def solution(mesh):
    in_specs = (
        P(("dp", "expert"), None),
        P(),
        P(),
        P("expert", None, "dp"),
        P("expert", None, "dp"),
        P("expert", "dp", None),
    )
    out_specs = P(("dp", "expert"), None)
    return jax.shard_map(shards, mesh=mesh, in_specs=in_specs, out_specs=out_specs, check_vma=False)
```

```python
import jax
import jax.numpy as jnp
from jax import lax
from jax.sharding import PartitionSpec as P

CHIP_ROWS = 96


def slot_tables(chosen, tok_count, my_index):
    owners = chosen // tok_count
    capacity = chosen.shape[1]
    is_mine = owners == my_index
    earlier = (
        jnp.arange(capacity, dtype=jnp.int32)[:, None]
        < jnp.arange(capacity, dtype=jnp.int32)[None, :]
    ).astype(jnp.bfloat16)
    ranks = jnp.dot(is_mine.astype(jnp.bfloat16), earlier, preferred_element_type=jnp.float32)
    return (owners, is_mine, ranks.astype(jnp.int32))

def dp_pairs(dp_count, shift):
    ny = dp_count // 2
    return [(y * 2 + c, ((y + shift) % ny) * 2 + c) for y in range(ny) for c in range(2)]


def sib_pairs(dp_count):
    return [(y * 2 + c, y * 2 + 1 - c) for y in range(dp_count // 2) for c in range(2)]


def gather_dp(x, dp_count):
    half = x.shape[1] // 2
    up = lax.ppermute(x, "dp", dp_pairs(dp_count, 1))
    dn = lax.ppermute(x, "dp", dp_pairs(dp_count, -1))
    sib = lax.ppermute(x, "dp", sib_pairs(dp_count))
    far_a = lax.ppermute(up[:, :half], "dp", dp_pairs(dp_count, 1))
    far_b = lax.ppermute(dn[:, half:], "dp", dp_pairs(dp_count, -1))
    far = jnp.concatenate([far_a, far_b], axis=1)
    s_up = lax.ppermute(up, "dp", sib_pairs(dp_count))
    s_dn = lax.ppermute(dn, "dp", sib_pairs(dp_count))
    s_far = lax.ppermute(far, "dp", sib_pairs(dp_count))
    return jnp.concatenate([x, sib, up, s_up, dn, s_dn, far, s_far], axis=0)


def scatter_dp(p, dp_count):
    rows = p.shape[0] // 8
    half = p.shape[1] // 2
    f32 = jnp.float32
    b = [p[i * rows:(i + 1) * rows] for i in range(8)]
    got_far = lax.ppermute(b[7], "dp", sib_pairs(dp_count))
    got = lax.ppermute(jnp.concatenate([b[1], b[3], b[5]], axis=0), "dp", sib_pairs(dp_count))
    g = [got[i * rows:(i + 1) * rows].astype(f32) for i in range(3)] + [got_far.astype(f32)]
    q_self = b[0].astype(f32) + g[0]
    q_up = b[2].astype(f32) + g[1]
    q_dn = b[4].astype(f32) + g[2]
    q_far = (b[6].astype(f32) + g[3]).astype(jnp.bfloat16)
    r_a = lax.ppermute(q_far[:, :half], "dp", dp_pairs(dp_count, 1)).astype(f32)
    r_b = lax.ppermute(q_far[:, half:], "dp", dp_pairs(dp_count, -1)).astype(f32)
    s_a = jnp.concatenate([q_dn[:, :half] + r_a, q_dn[:, half:]], axis=1).astype(jnp.bfloat16)
    s_b = jnp.concatenate([q_up[:, :half], q_up[:, half:] + r_b], axis=1).astype(jnp.bfloat16)
    a_a = lax.ppermute(s_a, "dp", dp_pairs(dp_count, 1)).astype(f32)
    a_b = lax.ppermute(s_b, "dp", dp_pairs(dp_count, -1)).astype(f32)
    return (q_self + a_a + a_b).astype(jnp.bfloat16)


def shards(tokens, chosen, combine_fixed, w_gate, w_up, w_down):
    dp_count = lax.axis_size("dp")
    ex_count = lax.axis_size("expert")
    worker_ordinal = dp_count * ex_count
    tok_count, model_width = tokens.shape
    expert_total, capacity = chosen.shape
    slot_count = min(tok_count, max(4, 2 * capacity // worker_ordinal))
    my_index = lax.axis_index("dp") * ex_count + lax.axis_index("expert")
    my_expert_idx = lax.axis_index("expert")
    owners, is_mine, ranks = slot_tables(chosen, tok_count, my_index)
    local_idx = chosen - owners * tok_count
    matches = is_mine[:, :, None] & (
        ranks[:, :, None] == jnp.arange(slot_count, dtype=jnp.int32)[None, None, :]
    )
    match_int = matches.astype(jnp.int32)
    source_idx = jnp.sum(match_int * local_idx[:, :, None], axis=1)
    present = jnp.sum(match_int, axis=1)
    scaled = combine_fixed.astype(jnp.float32) / 65536.0
    weights = jnp.sum(matches.astype(jnp.float32) * scaled[:, :, None], axis=1)
    send_rows = jnp.take(tokens, source_idx.reshape(-1), axis=0)
    send_rows = jnp.where(present.reshape(-1, 1) > 0, send_rows, jnp.zeros_like(send_rows))
    row_in = lax.all_to_all(send_rows, "expert", split_axis=0, concat_axis=0, tiled=True)
    def expert_rows(rows, w_g, w_u, w_d):
        picked = gather_dp(rows, dp_count)
        gate_act = jnp.dot(picked, w_g, preferred_element_type=jnp.float32)
        up_act = jnp.dot(picked, w_u, preferred_element_type=jnp.float32)
        hidden = (jax.nn.silu(gate_act) * up_act).astype(jnp.bfloat16)
        hidden = lax.optimization_barrier(hidden)
        result = jnp.dot(hidden, w_d, preferred_element_type=jnp.float32).astype(jnp.bfloat16)
        return scatter_dp(result, dp_count)

    dp_rows = owners // ex_count
    my_dp = lax.axis_index("dp")
    my_core = my_dp % 2
    counts = jnp.sum(
        (dp_rows[:, :, None] // 2 == jnp.arange(dp_count // 2, dtype=jnp.int32)[None, None, :]).astype(jnp.int32),
        axis=1,
    )
    chip_rows = min(2 * ex_count * slot_count, CHIP_ROWS)
    half_rows = chip_rows // 2
    slots = ex_count * slot_count
    row_owners = lax.dynamic_index_in_dim(owners, my_expert_idx, 0, keepdims=False)
    row_dp = row_owners // ex_count
    same_owner = row_owners[:, None] == row_owners[None, :]
    tri = (
        jnp.arange(capacity, dtype=jnp.int32)[:, None]
        < jnp.arange(capacity, dtype=jnp.int32)[None, :]
    )
    row_ranks = jnp.sum((same_owner & tri).astype(jnp.int32), axis=0)
    in_chip = (row_dp // 2) == (my_dp // 2)
    chip_pos = jnp.sum((in_chip[:, None] & tri).astype(jnp.int32), axis=0)
    slot_of = (row_owners % ex_count) * slot_count + row_ranks
    local_slot = ((row_dp % 2) * slots + slot_of + my_core * slots) % (2 * slots)
    wanted = my_core * half_rows + jnp.arange(half_rows, dtype=jnp.int32)
    pick_q = in_chip[None, :] & (chip_pos[None, :] == wanted[:, None])
    comp_src = jnp.sum(pick_q.astype(jnp.int32) * local_slot[None, :], axis=1)
    comp_ok = jnp.sum(pick_q.astype(jnp.int32), axis=1) > 0
    in_group = row_dp == my_dp
    pick_s = in_group[None, :] & (slot_of[None, :] == jnp.arange(slots, dtype=jnp.int32)[:, None])
    local_pos = (chip_pos + my_core * half_rows) % chip_rows
    back_src = jnp.sum(pick_s.astype(jnp.int32) * local_pos[None, :], axis=1)
    back_ok = jnp.sum(pick_s.astype(jnp.int32), axis=1) > 0

    def short_path(rows, w_g, w_u, w_d):
        both = jnp.concatenate([rows, lax.ppermute(rows, "dp", sib_pairs(dp_count))], axis=0)
        packed = jnp.take(both, comp_src, axis=0)
        packed = jnp.where(comp_ok[:, None], packed, jnp.zeros_like(packed))
        out = expert_rows(packed, w_g, w_u, w_d)
        full = jnp.concatenate([out, lax.ppermute(out, "dp", sib_pairs(dp_count))], axis=0)
        spread = jnp.take(full, back_src, axis=0)
        return jnp.where(back_ok[:, None], spread, jnp.zeros_like(spread))

    summed = lax.cond(
        jnp.max(counts) <= chip_rows, short_path, expert_rows, row_in, w_gate[0], w_up[0], w_down[0]
    )
    returned = lax.all_to_all(summed, "expert", split_axis=0, concat_axis=0, tiled=True)
    placed = (jnp.arange(tok_count, dtype=jnp.int32)[:, None] == source_idx.reshape(1, -1)) & (
        present.reshape(1, -1) > 0
    )
    mixing = jnp.where(placed, weights.reshape(1, -1), 0.0)
    mix_hi = mixing.astype(jnp.bfloat16)
    mix_lo = (mixing - mix_hi.astype(jnp.float32)).astype(jnp.bfloat16)
    mixed = jnp.dot(mix_hi, returned, preferred_element_type=jnp.float32) + jnp.dot(
        mix_lo, returned, preferred_element_type=jnp.float32
    )
    return mixed.astype(jnp.bfloat16)


def solution(mesh):
    in_specs = (
        P(("dp", "expert"), None),
        P(),
        P(),
        P("expert", None, "dp"),
        P("expert", None, "dp"),
        P("expert", "dp", None),
    )
    out_specs = P(("dp", "expert"), None)
    return jax.shard_map(shards, mesh=mesh, in_specs=in_specs, out_specs=out_specs, check_vma=False)
```

```python
import jax
import jax.numpy as jnp
from jax import lax
from jax.sharding import PartitionSpec as P

CHIP_ROWS = 96


def slot_tables(chosen, tok_count, my_index):
    owners = chosen // tok_count
    capacity = chosen.shape[1]
    is_mine = owners == my_index
    earlier = (
        jnp.arange(capacity, dtype=jnp.int32)[:, None]
        < jnp.arange(capacity, dtype=jnp.int32)[None, :]
    ).astype(jnp.bfloat16)
    ranks = jnp.dot(is_mine.astype(jnp.bfloat16), earlier, preferred_element_type=jnp.float32)
    return (owners, is_mine, ranks.astype(jnp.int32))

def dp_pairs(dp_count, shift):
    ny = dp_count // 2
    return [(y * 2 + c, ((y + shift) % ny) * 2 + c) for y in range(ny) for c in range(2)]


def sib_pairs(dp_count):
    return [(y * 2 + c, y * 2 + 1 - c) for y in range(dp_count // 2) for c in range(2)]


def gather_dp(x, dp_count, sib=None):
    half = x.shape[1] // 2
    up = lax.ppermute(x, "dp", dp_pairs(dp_count, 1))
    dn = lax.ppermute(x, "dp", dp_pairs(dp_count, -1))
    if sib is None:
        sib = lax.ppermute(x, "dp", sib_pairs(dp_count))
    far_a = lax.ppermute(up[:, :half], "dp", dp_pairs(dp_count, 1))
    far_b = lax.ppermute(dn[:, half:], "dp", dp_pairs(dp_count, -1))
    far = jnp.concatenate([far_a, far_b], axis=1)
    s_up = lax.ppermute(up, "dp", sib_pairs(dp_count))
    s_dn = lax.ppermute(dn, "dp", sib_pairs(dp_count))
    s_far = lax.ppermute(far, "dp", sib_pairs(dp_count))
    return jnp.concatenate([x, sib, up, s_up, dn, s_dn, far, s_far], axis=0)


def scatter_dp(p, dp_count):
    rows = p.shape[0] // 8
    half = p.shape[1] // 2
    f32 = jnp.float32
    b = [p[i * rows:(i + 1) * rows] for i in range(8)]
    got_far = lax.ppermute(b[7], "dp", sib_pairs(dp_count))
    got = lax.ppermute(jnp.concatenate([b[1], b[3], b[5]], axis=0), "dp", sib_pairs(dp_count))
    g = [got[i * rows:(i + 1) * rows].astype(f32) for i in range(3)] + [got_far.astype(f32)]
    q_self = b[0].astype(f32) + g[0]
    q_up = b[2].astype(f32) + g[1]
    q_dn = b[4].astype(f32) + g[2]
    q_far = (b[6].astype(f32) + g[3]).astype(jnp.bfloat16)
    r_a = lax.ppermute(q_far[:, :half], "dp", dp_pairs(dp_count, 1)).astype(f32)
    r_b = lax.ppermute(q_far[:, half:], "dp", dp_pairs(dp_count, -1)).astype(f32)
    s_a = jnp.concatenate([q_dn[:, :half] + r_a, q_dn[:, half:]], axis=1).astype(jnp.bfloat16)
    s_b = jnp.concatenate([q_up[:, :half], q_up[:, half:] + r_b], axis=1).astype(jnp.bfloat16)
    a_a = lax.ppermute(s_a, "dp", dp_pairs(dp_count, 1)).astype(f32)
    a_b = lax.ppermute(s_b, "dp", dp_pairs(dp_count, -1)).astype(f32)
    return (q_self + a_a + a_b).astype(jnp.bfloat16)


def shards(tokens, chosen, combine_fixed, w_gate, w_up, w_down):
    dp_count = lax.axis_size("dp")
    ex_count = lax.axis_size("expert")
    worker_ordinal = dp_count * ex_count
    tok_count, model_width = tokens.shape
    expert_total, capacity = chosen.shape
    slot_count = min(tok_count, max(4, 2 * capacity // worker_ordinal))
    my_index = lax.axis_index("dp") * ex_count + lax.axis_index("expert")
    my_expert_idx = lax.axis_index("expert")
    owners, is_mine, ranks = slot_tables(chosen, tok_count, my_index)
    local_idx = chosen - owners * tok_count
    matches = is_mine[:, :, None] & (
        ranks[:, :, None] == jnp.arange(slot_count, dtype=jnp.int32)[None, None, :]
    )
    match_int = matches.astype(jnp.int32)
    source_idx = jnp.sum(match_int * local_idx[:, :, None], axis=1)
    present = jnp.sum(match_int, axis=1)
    scaled = combine_fixed.astype(jnp.float32) / 65536.0
    weights = jnp.sum(matches.astype(jnp.float32) * scaled[:, :, None], axis=1)
    send_rows = jnp.take(tokens, source_idx.reshape(-1), axis=0)
    send_rows = jnp.where(present.reshape(-1, 1) > 0, send_rows, jnp.zeros_like(send_rows))
    row_in = lax.all_to_all(send_rows, "expert", split_axis=0, concat_axis=0, tiled=True)
    def expert_rows(rows, w_g, w_u, w_d, sib_rows=None):
        picked = gather_dp(rows, dp_count, sib_rows)
        gate_act = jnp.dot(picked, w_g, preferred_element_type=jnp.float32)
        up_act = jnp.dot(picked, w_u, preferred_element_type=jnp.float32)
        hidden = (jax.nn.silu(gate_act) * up_act).astype(jnp.bfloat16)
        hidden = lax.optimization_barrier(hidden)
        result = jnp.dot(hidden, w_d, preferred_element_type=jnp.float32).astype(jnp.bfloat16)
        return scatter_dp(result, dp_count)

    dp_rows = owners // ex_count
    my_dp = lax.axis_index("dp")
    my_core = my_dp % 2
    counts = jnp.sum(
        (dp_rows[:, :, None] // 2 == jnp.arange(dp_count // 2, dtype=jnp.int32)[None, None, :]).astype(jnp.int32),
        axis=1,
    )
    chip_rows = min(2 * ex_count * slot_count, CHIP_ROWS)
    half_rows = chip_rows // 2
    slots = ex_count * slot_count
    row_owners = lax.dynamic_index_in_dim(owners, my_expert_idx, 0, keepdims=False)
    row_dp = row_owners // ex_count
    same_owner = row_owners[:, None] == row_owners[None, :]
    tri = (
        jnp.arange(capacity, dtype=jnp.int32)[:, None]
        < jnp.arange(capacity, dtype=jnp.int32)[None, :]
    )
    row_ranks = jnp.sum((same_owner & tri).astype(jnp.int32), axis=0)
    in_chip = (row_dp // 2) == (my_dp // 2)
    chip_pos = jnp.sum((in_chip[:, None] & tri).astype(jnp.int32), axis=0)
    slot_of = (row_owners % ex_count) * slot_count + row_ranks
    local_slot = ((row_dp % 2) * slots + slot_of + my_core * slots) % (2 * slots)
    wanted = jnp.arange(chip_rows, dtype=jnp.int32)
    pick_q = in_chip[None, :] & (chip_pos[None, :] == wanted[:, None])
    comp_src = jnp.sum(pick_q.astype(jnp.int32) * local_slot[None, :], axis=1)
    comp_src = jnp.roll(comp_src.reshape(2, half_rows), -my_core, axis=0).reshape(-1)
    in_group = row_dp == my_dp
    pick_s = in_group[None, :] & (slot_of[None, :] == jnp.arange(slots, dtype=jnp.int32)[:, None])
    local_pos = (chip_pos + my_core * half_rows) % chip_rows
    back_src = jnp.sum(pick_s.astype(jnp.int32) * local_pos[None, :], axis=1)

    def short_path(rows, w_g, w_u, w_d):
        both = jnp.concatenate([rows, lax.ppermute(rows, "dp", sib_pairs(dp_count))], axis=0)
        packed = jnp.take(both, comp_src, axis=0)
        out = expert_rows(packed[:half_rows], w_g, w_u, w_d, packed[half_rows:])
        full = jnp.concatenate([out, lax.ppermute(out, "dp", sib_pairs(dp_count))], axis=0)
        return jnp.take(full, back_src, axis=0)

    summed = lax.cond(
        jnp.max(counts) <= chip_rows, short_path, expert_rows, row_in, w_gate[0], w_up[0], w_down[0]
    )
    returned = lax.all_to_all(summed, "expert", split_axis=0, concat_axis=0, tiled=True)
    placed = (jnp.arange(tok_count, dtype=jnp.int32)[:, None] == source_idx.reshape(1, -1)) & (
        present.reshape(1, -1) > 0
    )
    mixing = jnp.where(placed, weights.reshape(1, -1), 0.0)
    mix_hi = mixing.astype(jnp.bfloat16)
    mix_lo = (mixing - mix_hi.astype(jnp.float32)).astype(jnp.bfloat16)
    mixed = jnp.dot(mix_hi, returned, preferred_element_type=jnp.float32) + jnp.dot(
        mix_lo, returned, preferred_element_type=jnp.float32
    )
    return mixed.astype(jnp.bfloat16)


def solution(mesh):
    in_specs = (
        P(("dp", "expert"), None),
        P(),
        P(),
        P("expert", None, "dp"),
        P("expert", None, "dp"),
        P("expert", "dp", None),
    )
    out_specs = P(("dp", "expert"), None)
    return jax.shard_map(shards, mesh=mesh, in_specs=in_specs, out_specs=out_specs, check_vma=False)
```

```python
import jax
import jax.numpy as jnp
from jax import lax
from jax.sharding import PartitionSpec as P


def slot_tables(chosen, tok_count, my_index):
    owners = chosen // tok_count
    capacity = chosen.shape[1]
    is_mine = owners == my_index
    earlier = (
        jnp.arange(capacity, dtype=jnp.int32)[:, None]
        < jnp.arange(capacity, dtype=jnp.int32)[None, :]
    ).astype(jnp.bfloat16)
    ranks = jnp.dot(is_mine.astype(jnp.bfloat16), earlier, preferred_element_type=jnp.float32)
    return (owners, is_mine, ranks.astype(jnp.int32))

def dp_pairs(dp_count, shift):
    ny = dp_count // 2
    return [(y * 2 + c, ((y + shift) % ny) * 2 + c) for y in range(ny) for c in range(2)]


def sib_pairs(dp_count):
    return [(y * 2 + c, y * 2 + 1 - c) for y in range(dp_count // 2) for c in range(2)]


def gather_dp(x, dp_count):
    half = x.shape[1] // 2
    up = lax.ppermute(x, "dp", dp_pairs(dp_count, 1))
    dn = lax.ppermute(x, "dp", dp_pairs(dp_count, -1))
    sib = lax.ppermute(x, "dp", sib_pairs(dp_count))
    far_a = lax.ppermute(up[:, :half], "dp", dp_pairs(dp_count, 1))
    far_b = lax.ppermute(dn[:, half:], "dp", dp_pairs(dp_count, -1))
    far = jnp.concatenate([far_a, far_b], axis=1)
    s_up = lax.ppermute(up, "dp", sib_pairs(dp_count))
    s_dn = lax.ppermute(dn, "dp", sib_pairs(dp_count))
    s_far = lax.ppermute(far, "dp", sib_pairs(dp_count))
    return [x, sib, up, s_up, dn, s_dn, far, s_far]


def scatter_dp(p, dp_count):
    rows = p[0].shape[0]
    half = p[0].shape[1] // 2
    f32 = jnp.float32
    b = p
    got_far = lax.ppermute(b[7], "dp", sib_pairs(dp_count))
    got = lax.ppermute(jnp.concatenate([b[1], b[3], b[5]], axis=0), "dp", sib_pairs(dp_count))
    g = [got[i * rows:(i + 1) * rows].astype(f32) for i in range(3)] + [got_far.astype(f32)]
    q_self = b[0].astype(f32) + g[0]
    q_up = b[2].astype(f32) + g[1]
    q_dn = b[4].astype(f32) + g[2]
    q_far = (b[6].astype(f32) + g[3]).astype(jnp.bfloat16)
    r_a = lax.ppermute(q_far[:, :half], "dp", dp_pairs(dp_count, 1)).astype(f32)
    r_b = lax.ppermute(q_far[:, half:], "dp", dp_pairs(dp_count, -1)).astype(f32)
    s_a = jnp.concatenate([q_dn[:, :half] + r_a, q_dn[:, half:]], axis=1).astype(jnp.bfloat16)
    s_b = jnp.concatenate([q_up[:, :half], q_up[:, half:] + r_b], axis=1).astype(jnp.bfloat16)
    a_a = lax.ppermute(s_a, "dp", dp_pairs(dp_count, 1)).astype(f32)
    a_b = lax.ppermute(s_b, "dp", dp_pairs(dp_count, -1)).astype(f32)
    return (q_self + a_a + a_b).astype(jnp.bfloat16)


def shards(tokens, chosen, combine_fixed, w_gate, w_up, w_down):
    dp_count = lax.axis_size("dp")
    ex_count = lax.axis_size("expert")
    worker_ordinal = dp_count * ex_count
    tok_count, model_width = tokens.shape
    expert_total, capacity = chosen.shape
    slot_count = min(tok_count, max(4, 2 * capacity // worker_ordinal))
    my_index = lax.axis_index("dp") * ex_count + lax.axis_index("expert")
    owners, is_mine, ranks = slot_tables(chosen, tok_count, my_index)
    local_idx = chosen - owners * tok_count
    matches = is_mine[:, :, None] & (
        ranks[:, :, None] == jnp.arange(slot_count, dtype=jnp.int32)[None, None, :]
    )
    match_int = matches.astype(jnp.int32)
    source_idx = jnp.sum(match_int * local_idx[:, :, None], axis=1)
    present = jnp.sum(match_int, axis=1)
    scaled = combine_fixed.astype(jnp.float32) / 65536.0
    weights = jnp.sum(matches.astype(jnp.float32) * scaled[:, :, None], axis=1)
    send_rows = jnp.take(tokens, source_idx.reshape(-1), axis=0)
    send_rows = jnp.where(present.reshape(-1, 1) > 0, send_rows, jnp.zeros_like(send_rows))
    row_in = lax.all_to_all(send_rows, "expert", split_axis=0, concat_axis=0, tiled=True)
    blocks = gather_dp(row_in, dp_count)
    rows = row_in.shape[0]
    hidden = []
    for part in (blocks[:6], blocks[6:]):
        picked = jnp.concatenate(part, axis=0)
        gate_act = jnp.dot(picked, w_gate[0], preferred_element_type=jnp.float32)
        up_act = jnp.dot(picked, w_up[0], preferred_element_type=jnp.float32)
        hidden.append((jax.nn.silu(gate_act) * up_act).astype(jnp.bfloat16))
    hidden = lax.optimization_barrier(jnp.concatenate(hidden, axis=0))
    hb = [hidden[i * rows:(i + 1) * rows] for i in range(8)]
    result = [None] * 8
    for group in ((1, 3, 5, 7), (0, 2, 4, 6)):
        out = jnp.dot(
            jnp.concatenate([hb[i] for i in group], axis=0), w_down[0], preferred_element_type=jnp.float32
        ).astype(jnp.bfloat16)
        for n, i in enumerate(group):
            result[i] = out[n * rows:(n + 1) * rows]
    summed = scatter_dp(result, dp_count)
    returned = lax.all_to_all(summed, "expert", split_axis=0, concat_axis=0, tiled=True)
    placed = (jnp.arange(tok_count, dtype=jnp.int32)[:, None] == source_idx.reshape(1, -1)) & (
        present.reshape(1, -1) > 0
    )
    mixing = jnp.where(placed, weights.reshape(1, -1), 0.0)
    mix_hi = mixing.astype(jnp.bfloat16)
    mix_lo = (mixing - mix_hi.astype(jnp.float32)).astype(jnp.bfloat16)
    mixed = jnp.dot(mix_hi, returned, preferred_element_type=jnp.float32) + jnp.dot(
        mix_lo, returned, preferred_element_type=jnp.float32
    )
    return mixed.astype(jnp.bfloat16)


def solution(mesh):
    in_specs = (
        P(("dp", "expert"), None),
        P(),
        P(),
        P("expert", None, "dp"),
        P("expert", None, "dp"),
        P("expert", "dp", None),
    )
    out_specs = P(("dp", "expert"), None)
    return jax.shard_map(shards, mesh=mesh, in_specs=in_specs, out_specs=out_specs, check_vma=False)
```

```python
import jax
import jax.numpy as jnp
from jax import lax
from jax.sharding import PartitionSpec as P


def slot_tables(chosen, tok_count, my_index):
    owners = chosen // tok_count
    capacity = chosen.shape[1]
    is_mine = owners == my_index
    earlier = (
        jnp.arange(capacity, dtype=jnp.int32)[:, None]
        < jnp.arange(capacity, dtype=jnp.int32)[None, :]
    ).astype(jnp.bfloat16)
    ranks = jnp.dot(is_mine.astype(jnp.bfloat16), earlier, preferred_element_type=jnp.float32)
    return (owners, is_mine, ranks.astype(jnp.int32))

def dp_pairs(dp_count, shift):
    ny = dp_count // 2
    return [(y * 2 + c, ((y + shift) % ny) * 2 + c) for y in range(ny) for c in range(2)]


def sib_pairs(dp_count):
    return [(y * 2 + c, y * 2 + 1 - c) for y in range(dp_count // 2) for c in range(2)]


def gather_dp(x, dp_count):
    half = x.shape[1] // 2
    up = lax.ppermute(x, "dp", dp_pairs(dp_count, 1))
    dn = lax.ppermute(x, "dp", dp_pairs(dp_count, -1))
    sib = lax.ppermute(x, "dp", sib_pairs(dp_count))
    far_a = lax.ppermute(up[:, :half], "dp", dp_pairs(dp_count, 1))
    far_b = lax.ppermute(dn[:, half:], "dp", dp_pairs(dp_count, -1))
    far = jnp.concatenate([far_a, far_b], axis=1)
    s_up = lax.ppermute(up, "dp", sib_pairs(dp_count))
    s_dn = lax.ppermute(dn, "dp", sib_pairs(dp_count))
    s_far = lax.ppermute(far, "dp", sib_pairs(dp_count))
    return [x, sib, up, s_up, dn, s_dn, far, s_far]


def scatter_dp(p, dp_count):
    rows = p[0].shape[0]
    half = p[0].shape[1] // 2
    f32 = jnp.float32
    b = p
    got_far = lax.ppermute(b[7], "dp", sib_pairs(dp_count))
    got = lax.ppermute(jnp.concatenate([b[1], b[3], b[5]], axis=0), "dp", sib_pairs(dp_count))
    g = [got[i * rows:(i + 1) * rows].astype(f32) for i in range(3)] + [got_far.astype(f32)]
    q_self = b[0].astype(f32) + g[0]
    q_up = b[2].astype(f32) + g[1]
    q_dn = b[4].astype(f32) + g[2]
    q_far = (b[6].astype(f32) + g[3]).astype(jnp.bfloat16)
    r_a = lax.ppermute(q_far[:, :half], "dp", dp_pairs(dp_count, 1)).astype(f32)
    r_b = lax.ppermute(q_far[:, half:], "dp", dp_pairs(dp_count, -1)).astype(f32)
    s_a = jnp.concatenate([q_dn[:, :half] + r_a, q_dn[:, half:]], axis=1).astype(jnp.bfloat16)
    s_b = jnp.concatenate([q_up[:, :half], q_up[:, half:] + r_b], axis=1).astype(jnp.bfloat16)
    a_a = lax.ppermute(s_a, "dp", dp_pairs(dp_count, 1)).astype(f32)
    a_b = lax.ppermute(s_b, "dp", dp_pairs(dp_count, -1)).astype(f32)
    return (q_self + a_a + a_b).astype(jnp.bfloat16)


def shards(tokens, chosen, combine_fixed, w_gate, w_up, w_down):
    dp_count = lax.axis_size("dp")
    ex_count = lax.axis_size("expert")
    worker_ordinal = dp_count * ex_count
    tok_count, model_width = tokens.shape
    expert_total, capacity = chosen.shape
    slot_count = min(tok_count, max(4, 2 * capacity // worker_ordinal))
    my_index = lax.axis_index("dp") * ex_count + lax.axis_index("expert")
    owners, is_mine, ranks = slot_tables(chosen, tok_count, my_index)
    local_idx = chosen - owners * tok_count
    matches = is_mine[:, :, None] & (
        ranks[:, :, None] == jnp.arange(slot_count, dtype=jnp.int32)[None, None, :]
    )
    match_int = matches.astype(jnp.int32)
    source_idx = jnp.sum(match_int * local_idx[:, :, None], axis=1)
    present = jnp.sum(match_int, axis=1)
    scaled = combine_fixed.astype(jnp.float32) / 65536.0
    weights = jnp.sum(matches.astype(jnp.float32) * scaled[:, :, None], axis=1)
    send_rows = jnp.take(tokens, source_idx.reshape(-1), axis=0)
    send_rows = jnp.where(present.reshape(-1, 1) > 0, send_rows, jnp.zeros_like(send_rows))
    row_in = lax.all_to_all(send_rows, "expert", split_axis=0, concat_axis=0, tiled=True)
    blocks = gather_dp(row_in, dp_count)
    rows = row_in.shape[0]
    hidden = []
    for part in (blocks[:6], blocks[6:]):
        picked = jnp.concatenate(part, axis=0)
        gate_act = jnp.dot(picked, w_gate[0], preferred_element_type=jnp.float32)
        up_act = jnp.dot(picked, w_up[0], preferred_element_type=jnp.float32)
        hidden.append((jax.nn.silu(gate_act) * up_act).astype(jnp.bfloat16))
    hidden = lax.optimization_barrier(jnp.concatenate(hidden, axis=0))
    hb = [hidden[i * rows:(i + 1) * rows] for i in range(8)]
    result = [None] * 8
    for group in ((7,), (6,), (1, 3, 5), (0, 2, 4)):
        out = jnp.dot(
            jnp.concatenate([hb[i] for i in group], axis=0), w_down[0], preferred_element_type=jnp.float32
        ).astype(jnp.bfloat16)
        for n, i in enumerate(group):
            result[i] = out[n * rows:(n + 1) * rows]
    summed = scatter_dp(result, dp_count)
    returned = lax.all_to_all(summed, "expert", split_axis=0, concat_axis=0, tiled=True)
    placed = (jnp.arange(tok_count, dtype=jnp.int32)[:, None] == source_idx.reshape(1, -1)) & (
        present.reshape(1, -1) > 0
    )
    mixing = jnp.where(placed, weights.reshape(1, -1), 0.0)
    mix_hi = mixing.astype(jnp.bfloat16)
    mix_lo = (mixing - mix_hi.astype(jnp.float32)).astype(jnp.bfloat16)
    mixed = jnp.dot(mix_hi, returned, preferred_element_type=jnp.float32) + jnp.dot(
        mix_lo, returned, preferred_element_type=jnp.float32
    )
    return mixed.astype(jnp.bfloat16)


def solution(mesh):
    in_specs = (
        P(("dp", "expert"), None),
        P(),
        P(),
        P("expert", None, "dp"),
        P("expert", None, "dp"),
        P("expert", "dp", None),
    )
    out_specs = P(("dp", "expert"), None)
    return jax.shard_map(shards, mesh=mesh, in_specs=in_specs, out_specs=out_specs, check_vma=False)
```

```python
import jax
import jax.numpy as jnp
from jax import lax
from jax.sharding import PartitionSpec as P


def slot_tables(chosen, tok_count, my_index):
    owners = chosen // tok_count
    capacity = chosen.shape[1]
    is_mine = owners == my_index
    earlier = (
        jnp.arange(capacity, dtype=jnp.int32)[:, None]
        < jnp.arange(capacity, dtype=jnp.int32)[None, :]
    ).astype(jnp.bfloat16)
    ranks = jnp.dot(is_mine.astype(jnp.bfloat16), earlier, preferred_element_type=jnp.float32)
    return (owners, is_mine, ranks.astype(jnp.int32))

def dp_pairs(dp_count, shift):
    ny = dp_count // 2
    return [(y * 2 + c, ((y + shift) % ny) * 2 + c) for y in range(ny) for c in range(2)]


def sib_pairs(dp_count):
    return [(y * 2 + c, y * 2 + 1 - c) for y in range(dp_count // 2) for c in range(2)]


def gather_dp(x, dp_count):
    half = x.shape[1] // 2
    up = lax.ppermute(x, "dp", dp_pairs(dp_count, 1))
    dn = lax.ppermute(x, "dp", dp_pairs(dp_count, -1))
    sib = lax.ppermute(x, "dp", sib_pairs(dp_count))
    far_a = lax.ppermute(up[:, :half], "dp", dp_pairs(dp_count, 1))
    far_b = lax.ppermute(dn[:, half:], "dp", dp_pairs(dp_count, -1))
    far = jnp.concatenate([far_a, far_b], axis=1)
    s_up = lax.ppermute(up, "dp", sib_pairs(dp_count))
    s_dn = lax.ppermute(dn, "dp", sib_pairs(dp_count))
    s_far = lax.ppermute(far, "dp", sib_pairs(dp_count))
    return [x, sib, up, s_up, dn, s_dn, far, s_far]


def scatter_dp(p, dp_count):
    rows = p[0].shape[0]
    half = p[0].shape[1] // 2
    f32 = jnp.float32
    b = p
    got_far = lax.ppermute(b[7], "dp", sib_pairs(dp_count))
    got = lax.ppermute(jnp.concatenate([b[1], b[3], b[5]], axis=0), "dp", sib_pairs(dp_count))
    g = [got[i * rows:(i + 1) * rows].astype(f32) for i in range(3)] + [got_far.astype(f32)]
    q_self = b[0].astype(f32) + g[0]
    q_up = b[2].astype(f32) + g[1]
    q_dn = b[4].astype(f32) + g[2]
    q_far = (b[6].astype(f32) + g[3]).astype(jnp.bfloat16)
    r_a = lax.ppermute(q_far[:, :half], "dp", dp_pairs(dp_count, 1)).astype(f32)
    r_b = lax.ppermute(q_far[:, half:], "dp", dp_pairs(dp_count, -1)).astype(f32)
    s_a = jnp.concatenate([q_dn[:, :half] + r_a, q_dn[:, half:]], axis=1).astype(jnp.bfloat16)
    s_b = jnp.concatenate([q_up[:, :half], q_up[:, half:] + r_b], axis=1).astype(jnp.bfloat16)
    a_a = lax.ppermute(s_a, "dp", dp_pairs(dp_count, 1)).astype(f32)
    a_b = lax.ppermute(s_b, "dp", dp_pairs(dp_count, -1)).astype(f32)
    return (q_self + a_a + a_b).astype(jnp.bfloat16)


def shards(tokens, chosen, combine_fixed, w_gate, w_up, w_down):
    dp_count = lax.axis_size("dp")
    ex_count = lax.axis_size("expert")
    worker_ordinal = dp_count * ex_count
    tok_count, model_width = tokens.shape
    expert_total, capacity = chosen.shape
    slot_count = min(tok_count, max(4, 2 * capacity // worker_ordinal))
    my_index = lax.axis_index("dp") * ex_count + lax.axis_index("expert")
    owners, is_mine, ranks = slot_tables(chosen, tok_count, my_index)
    local_idx = chosen - owners * tok_count
    matches = is_mine[:, :, None] & (
        ranks[:, :, None] == jnp.arange(slot_count, dtype=jnp.int32)[None, None, :]
    )
    match_int = matches.astype(jnp.int32)
    source_idx = jnp.sum(match_int * local_idx[:, :, None], axis=1)
    present = jnp.sum(match_int, axis=1)
    scaled = combine_fixed.astype(jnp.float32) / 65536.0
    weights = jnp.sum(matches.astype(jnp.float32) * scaled[:, :, None], axis=1)
    send_rows = jnp.take(tokens, source_idx.reshape(-1), axis=0)
    send_rows = jnp.where(present.reshape(-1, 1) > 0, send_rows, jnp.zeros_like(send_rows))
    row_in = lax.all_to_all(send_rows, "expert", split_axis=0, concat_axis=0, tiled=True)
    blocks = gather_dp(row_in, dp_count)
    rows = row_in.shape[0]
    hidden = []
    for part in (blocks[:6], blocks[6:]):
        picked = jnp.concatenate(part, axis=0)
        gate_act = jnp.dot(picked, w_gate[0], preferred_element_type=jnp.float32)
        up_act = jnp.dot(picked, w_up[0], preferred_element_type=jnp.float32)
        hidden.append((jax.nn.silu(gate_act) * up_act).astype(jnp.bfloat16))
    hidden = lax.optimization_barrier(jnp.concatenate(hidden, axis=0))
    hb = [hidden[i * rows:(i + 1) * rows] for i in range(8)]
    result = [None] * 8
    for group in ((1, 3, 5, 7), (0, 2, 4, 6)):
        out = jnp.dot(
            jnp.concatenate([hb[i] for i in group], axis=0), w_down[0], preferred_element_type=jnp.float32
        ).astype(jnp.bfloat16)
        for n, i in enumerate(group):
            result[i] = out[n * rows:(n + 1) * rows]
    summed = scatter_dp(result, dp_count)
    summed = summed.reshape(ex_count, slot_count, model_width)
    returned = lax.all_to_all(summed, "expert", split_axis=0, concat_axis=0, tiled=True)
    placed = (jnp.arange(tok_count, dtype=jnp.int32)[:, None] == source_idx.reshape(1, -1)) & (
        present.reshape(1, -1) > 0
    )
    mixing = jnp.where(placed, weights.reshape(1, -1), 0.0)
    mix_hi = mixing.astype(jnp.bfloat16)
    mix_lo = (mixing - mix_hi.astype(jnp.float32)).astype(jnp.bfloat16)
    dims = (((1, 2), (0, 1)), ((), ()))
    mix_hi = mix_hi.reshape(tok_count, ex_count, slot_count)
    mix_lo = mix_lo.reshape(tok_count, ex_count, slot_count)
    mixed = lax.dot_general(mix_hi, returned, dims, preferred_element_type=jnp.float32) + lax.dot_general(
        mix_lo, returned, dims, preferred_element_type=jnp.float32
    )
    return mixed.astype(jnp.bfloat16)


def solution(mesh):
    in_specs = (
        P(("dp", "expert"), None),
        P(),
        P(),
        P("expert", None, "dp"),
        P("expert", None, "dp"),
        P("expert", "dp", None),
    )
    out_specs = P(("dp", "expert"), None)
    return jax.shard_map(shards, mesh=mesh, in_specs=in_specs, out_specs=out_specs, check_vma=False)
```

```python
import jax
import jax.numpy as jnp
from jax import lax
from jax.sharding import PartitionSpec as P


def slot_tables(chosen, tok_count, my_index):
    owners = chosen // tok_count
    capacity = chosen.shape[1]
    is_mine = owners == my_index
    earlier = (
        jnp.arange(capacity, dtype=jnp.int32)[:, None]
        < jnp.arange(capacity, dtype=jnp.int32)[None, :]
    ).astype(jnp.bfloat16)
    ranks = jnp.dot(is_mine.astype(jnp.bfloat16), earlier, preferred_element_type=jnp.float32)
    return (owners, is_mine, ranks.astype(jnp.int32))

def dp_pairs(dp_count, shift):
    ny = dp_count // 2
    return [(y * 2 + c, ((y + shift) % ny) * 2 + c) for y in range(ny) for c in range(2)]


def sib_pairs(dp_count):
    return [(y * 2 + c, y * 2 + 1 - c) for y in range(dp_count // 2) for c in range(2)]


def gather_dp(x, dp_count):
    half = x.shape[1] // 2
    up = lax.ppermute(x, "dp", dp_pairs(dp_count, 1))
    dn = lax.ppermute(x, "dp", dp_pairs(dp_count, -1))
    sib = lax.ppermute(x, "dp", sib_pairs(dp_count))
    far_a = lax.ppermute(up[:, :half], "dp", dp_pairs(dp_count, 1))
    far_b = lax.ppermute(dn[:, half:], "dp", dp_pairs(dp_count, -1))
    far = jnp.concatenate([far_a, far_b], axis=1)
    s_up = lax.ppermute(up, "dp", sib_pairs(dp_count))
    s_dn = lax.ppermute(dn, "dp", sib_pairs(dp_count))
    s_far = lax.ppermute(far, "dp", sib_pairs(dp_count))
    return [x, sib, up, s_up, dn, s_dn, far, s_far]


def scatter_dp(p, dp_count):
    rows = p[0].shape[0]
    half = p[0].shape[1] // 2
    f32 = jnp.float32
    b = p
    got_far = lax.ppermute(b[7], "dp", sib_pairs(dp_count))
    got = lax.ppermute(jnp.concatenate([b[1], b[3], b[5]], axis=0), "dp", sib_pairs(dp_count))
    g = [got[i * rows:(i + 1) * rows].astype(f32) for i in range(3)]
    own_far, sib_far = lax.optimization_barrier((b[6], got_far))
    q_far = (own_far.astype(f32) + sib_far.astype(f32)).astype(jnp.bfloat16)
    q_self = b[0].astype(f32) + g[0]
    q_up = b[2].astype(f32) + g[1]
    q_dn = b[4].astype(f32) + g[2]
    r_a = lax.ppermute(q_far[:, :half], "dp", dp_pairs(dp_count, 1)).astype(f32)
    r_b = lax.ppermute(q_far[:, half:], "dp", dp_pairs(dp_count, -1)).astype(f32)
    s_a = jnp.concatenate([q_dn[:, :half] + r_a, q_dn[:, half:]], axis=1).astype(jnp.bfloat16)
    s_b = jnp.concatenate([q_up[:, :half], q_up[:, half:] + r_b], axis=1).astype(jnp.bfloat16)
    a_a = lax.ppermute(s_a, "dp", dp_pairs(dp_count, 1)).astype(f32)
    a_b = lax.ppermute(s_b, "dp", dp_pairs(dp_count, -1)).astype(f32)
    return (q_self + a_a + a_b).astype(jnp.bfloat16)


def shards(tokens, chosen, combine_fixed, w_gate, w_up, w_down):
    dp_count = lax.axis_size("dp")
    ex_count = lax.axis_size("expert")
    worker_ordinal = dp_count * ex_count
    tok_count, model_width = tokens.shape
    expert_total, capacity = chosen.shape
    slot_count = min(tok_count, max(4, 2 * capacity // worker_ordinal))
    my_index = lax.axis_index("dp") * ex_count + lax.axis_index("expert")
    owners, is_mine, ranks = slot_tables(chosen, tok_count, my_index)
    local_idx = chosen - owners * tok_count
    matches = is_mine[:, :, None] & (
        ranks[:, :, None] == jnp.arange(slot_count, dtype=jnp.int32)[None, None, :]
    )
    match_int = matches.astype(jnp.int32)
    source_idx = jnp.sum(match_int * local_idx[:, :, None], axis=1)
    present = jnp.sum(match_int, axis=1)
    scaled = combine_fixed.astype(jnp.float32) / 65536.0
    weights = jnp.sum(matches.astype(jnp.float32) * scaled[:, :, None], axis=1)
    send_rows = jnp.take(tokens, source_idx.reshape(-1), axis=0)
    send_rows = jnp.where(present.reshape(-1, 1) > 0, send_rows, jnp.zeros_like(send_rows))
    row_in = lax.all_to_all(send_rows, "expert", split_axis=0, concat_axis=0, tiled=True)
    blocks = gather_dp(row_in, dp_count)
    rows = row_in.shape[0]
    hidden = []
    for part in (blocks[:6], blocks[6:]):
        picked = jnp.concatenate(part, axis=0)
        gate_act = jnp.dot(picked, w_gate[0], preferred_element_type=jnp.float32)
        up_act = jnp.dot(picked, w_up[0], preferred_element_type=jnp.float32)
        hidden.append((jax.nn.silu(gate_act) * up_act).astype(jnp.bfloat16))
    hidden = lax.optimization_barrier(jnp.concatenate(hidden, axis=0))
    hb = [hidden[i * rows:(i + 1) * rows] for i in range(8)]
    result = [None] * 8
    for group in ((1, 3, 5, 7), (0, 2, 4, 6)):
        out = jnp.dot(
            jnp.concatenate([hb[i] for i in group], axis=0), w_down[0], preferred_element_type=jnp.float32
        ).astype(jnp.bfloat16)
        for n, i in enumerate(group):
            result[i] = out[n * rows:(n + 1) * rows]
    summed = scatter_dp(result, dp_count)
    summed = summed.reshape(ex_count, slot_count, model_width)
    returned = lax.all_to_all(summed, "expert", split_axis=0, concat_axis=0, tiled=True)
    placed = (jnp.arange(tok_count, dtype=jnp.int32)[:, None] == source_idx.reshape(1, -1)) & (
        present.reshape(1, -1) > 0
    )
    mixing = jnp.where(placed, weights.reshape(1, -1), 0.0)
    mix_hi = mixing.astype(jnp.bfloat16)
    mix_lo = (mixing - mix_hi.astype(jnp.float32)).astype(jnp.bfloat16)
    dims = (((1, 2), (0, 1)), ((), ()))
    mix_hi = mix_hi.reshape(tok_count, ex_count, slot_count)
    mix_lo = mix_lo.reshape(tok_count, ex_count, slot_count)
    mixed = lax.dot_general(mix_hi, returned, dims, preferred_element_type=jnp.float32) + lax.dot_general(
        mix_lo, returned, dims, preferred_element_type=jnp.float32
    )
    return mixed.astype(jnp.bfloat16)


def solution(mesh):
    in_specs = (
        P(("dp", "expert"), None),
        P(),
        P(),
        P("expert", None, "dp"),
        P("expert", None, "dp"),
        P("expert", "dp", None),
    )
    out_specs = P(("dp", "expert"), None)
    return jax.shard_map(shards, mesh=mesh, in_specs=in_specs, out_specs=out_specs, check_vma=False)
```

```python
import jax
import jax.numpy as jnp
from jax import lax
from jax.sharding import PartitionSpec as P


def slot_tables(chosen, tok_count, my_index):
    owners = chosen // tok_count
    capacity = chosen.shape[1]
    is_mine = owners == my_index
    earlier = (
        jnp.arange(capacity, dtype=jnp.int32)[:, None]
        < jnp.arange(capacity, dtype=jnp.int32)[None, :]
    ).astype(jnp.bfloat16)
    ranks = jnp.dot(is_mine.astype(jnp.bfloat16), earlier, preferred_element_type=jnp.float32)
    return (owners, is_mine, ranks.astype(jnp.int32))


def dp_pairs(dp_count, shift):
    ny = dp_count // 2
    return [(y * 2 + c, ((y + shift) % ny) * 2 + c) for y in range(ny) for c in range(2)]


def sib_pairs(dp_count):
    return [(y * 2 + c, y * 2 + 1 - c) for y in range(dp_count // 2) for c in range(2)]


def gather_dp(x, dp_count):
    half = x.shape[1] // 2
    up = lax.ppermute(x, "dp", dp_pairs(dp_count, 1))
    dn = lax.ppermute(x, "dp", dp_pairs(dp_count, -1))
    sib = lax.ppermute(x, "dp", sib_pairs(dp_count))
    far_a = lax.ppermute(up[:, :half], "dp", dp_pairs(dp_count, 1))
    far_b = lax.ppermute(dn[:, half:], "dp", dp_pairs(dp_count, -1))
    far = jnp.concatenate([far_a, far_b], axis=1)
    s_up = lax.ppermute(up, "dp", sib_pairs(dp_count))
    s_dn = lax.ppermute(dn, "dp", sib_pairs(dp_count))
    s_far = lax.ppermute(far, "dp", sib_pairs(dp_count))
    return [x, sib, up, s_up, dn, s_dn, far, s_far]


def scatter_dp(p, dp_count):
    rows = p[0].shape[0]
    half = p[0].shape[1] // 2
    f32 = jnp.float32
    b = p
    got_far = lax.ppermute(b[7], "dp", sib_pairs(dp_count))
    got = lax.ppermute(jnp.concatenate([b[1], b[3], b[5]], axis=0), "dp", sib_pairs(dp_count))
    g = [got[i * rows:(i + 1) * rows].astype(f32) for i in range(3)]
    own_far, sib_far = lax.optimization_barrier((b[6], got_far))
    q_far = (own_far.astype(f32) + sib_far.astype(f32)).astype(jnp.bfloat16)
    q_self = b[0].astype(f32) + g[0]
    q_up = b[2].astype(f32) + g[1]
    q_dn = b[4].astype(f32) + g[2]
    r_a = lax.ppermute(q_far[:, :half], "dp", dp_pairs(dp_count, 1)).astype(f32)
    r_b = lax.ppermute(q_far[:, half:], "dp", dp_pairs(dp_count, -1)).astype(f32)
    s_a = jnp.concatenate([q_dn[:, :half] + r_a, q_dn[:, half:]], axis=1).astype(jnp.bfloat16)
    s_b = jnp.concatenate([q_up[:, :half], q_up[:, half:] + r_b], axis=1).astype(jnp.bfloat16)
    a_a = lax.ppermute(s_a, "dp", dp_pairs(dp_count, 1)).astype(f32)
    a_b = lax.ppermute(s_b, "dp", dp_pairs(dp_count, -1)).astype(f32)
    return (q_self + a_a + a_b).astype(jnp.bfloat16)


def layer(tokens, chosen, combine_fixed, w_gate, w_up, w_down):
    dp_count = lax.axis_size("dp")
    ex_count = lax.axis_size("expert")
    worker_ordinal = dp_count * ex_count
    tok_count, model_width = tokens.shape
    _, capacity = chosen.shape
    slot_count = min(tok_count, max(4, 2 * capacity // worker_ordinal))
    my_index = lax.axis_index("dp") * ex_count + lax.axis_index("expert")
    owners, is_mine, ranks = slot_tables(chosen, tok_count, my_index)
    local_idx = chosen - owners * tok_count
    matches = is_mine[:, :, None] & (
        ranks[:, :, None] == jnp.arange(slot_count, dtype=jnp.int32)[None, None, :]
    )
    match_int = matches.astype(jnp.int32)
    source_idx = jnp.sum(match_int * local_idx[:, :, None], axis=1)
    present = jnp.sum(match_int, axis=1)
    scaled = combine_fixed.astype(jnp.float32) / 65536.0
    weights = jnp.sum(matches.astype(jnp.float32) * scaled[:, :, None], axis=1)
    send_rows = jnp.take(tokens, source_idx.reshape(-1), axis=0)
    send_rows = jnp.where(present.reshape(-1, 1) > 0, send_rows, jnp.zeros_like(send_rows))
    row_in = lax.all_to_all(send_rows, "expert", split_axis=0, concat_axis=0, tiled=True)
    blocks = gather_dp(row_in, dp_count)
    rows = row_in.shape[0]
    hidden = []
    for part in (blocks[:6], blocks[6:]):
        picked = jnp.concatenate(part, axis=0)
        gate_act = jnp.dot(picked, w_gate[0], preferred_element_type=jnp.float32)
        up_act = jnp.dot(picked, w_up[0], preferred_element_type=jnp.float32)
        hidden.append((jax.nn.silu(gate_act) * up_act).astype(jnp.bfloat16))
    hidden = lax.optimization_barrier(jnp.concatenate(hidden, axis=0))
    hb = [hidden[i * rows:(i + 1) * rows] for i in range(8)]
    result = [None] * 8
    for group in ((1, 3, 5, 7), (0, 2, 4, 6)):
        out = jnp.dot(
            jnp.concatenate([hb[i] for i in group], axis=0), w_down[0], preferred_element_type=jnp.float32
        ).astype(jnp.bfloat16)
        for n, i in enumerate(group):
            result[i] = out[n * rows:(n + 1) * rows]
    summed = scatter_dp(result, dp_count)
    summed = summed.reshape(ex_count, slot_count, model_width)
    returned = lax.all_to_all(summed, "expert", split_axis=0, concat_axis=0, tiled=True)
    placed = (jnp.arange(tok_count, dtype=jnp.int32)[:, None] == source_idx.reshape(1, -1)) & (
        present.reshape(1, -1) > 0
    )
    mixing = jnp.where(placed, weights.reshape(1, -1), 0.0)
    mix_hi = mixing.astype(jnp.bfloat16)
    mix_lo = (mixing - mix_hi.astype(jnp.float32)).astype(jnp.bfloat16)
    dims = (((1, 2), (0, 1)), ((), ()))
    mix_hi = mix_hi.reshape(tok_count, ex_count, slot_count)
    mix_lo = mix_lo.reshape(tok_count, ex_count, slot_count)
    mixed = lax.dot_general(mix_hi, returned, dims, preferred_element_type=jnp.float32) + lax.dot_general(
        mix_lo, returned, dims, preferred_element_type=jnp.float32
    )
    return mixed.astype(jnp.bfloat16)


def solution(mesh):
    in_specs = (
        P(("dp", "expert"), None),
        P(),
        P(),
        P("expert", None, "dp"),
        P("expert", None, "dp"),
        P("expert", "dp", None),
    )
    out_specs = P(("dp", "expert"), None)
    return jax.shard_map(layer, mesh=mesh, in_specs=in_specs, out_specs=out_specs, check_vma=False)
```

```python
import jax
import jax.numpy as jnp
from jax import lax
from jax.sharding import PartitionSpec as P


def slot_tables(chosen, tok_count, my_index):
    owners = chosen // tok_count
    capacity = chosen.shape[1]
    is_mine = owners == my_index
    earlier = (
        jnp.arange(capacity, dtype=jnp.int32)[:, None]
        < jnp.arange(capacity, dtype=jnp.int32)[None, :]
    ).astype(jnp.bfloat16)
    ranks = jnp.dot(is_mine.astype(jnp.bfloat16), earlier, preferred_element_type=jnp.float32)
    return (owners, is_mine, ranks.astype(jnp.int32))


def dp_pairs(dp_count, shift):
    ny = dp_count // 2
    return [(y * 2 + c, ((y + shift) % ny) * 2 + c) for y in range(ny) for c in range(2)]


def sib_pairs(dp_count):
    return [(y * 2 + c, y * 2 + 1 - c) for y in range(dp_count // 2) for c in range(2)]


def gather_dp(x, dp_count):
    half = x.shape[1] // 2
    up = lax.ppermute(x, "dp", dp_pairs(dp_count, 1))
    dn = lax.ppermute(x, "dp", dp_pairs(dp_count, -1))
    sib = lax.ppermute(x, "dp", sib_pairs(dp_count))
    far_a = lax.ppermute(up[:, :half], "dp", dp_pairs(dp_count, 1))
    far_b = lax.ppermute(dn[:, half:], "dp", dp_pairs(dp_count, -1))
    far = jnp.concatenate([far_a, far_b], axis=1)
    s_up = lax.ppermute(up, "dp", sib_pairs(dp_count))
    s_dn = lax.ppermute(dn, "dp", sib_pairs(dp_count))
    s_far = lax.ppermute(far, "dp", sib_pairs(dp_count))
    return [x, sib, up, s_up, dn, s_dn, far, s_far]


def scatter_dp(p, dp_count):
    rows = p[0].shape[0]
    half = p[0].shape[1] // 2
    f32 = jnp.float32
    b = p
    got_far = lax.ppermute(b[7], "dp", sib_pairs(dp_count))
    got = lax.ppermute(jnp.concatenate([b[1], b[3], b[5]], axis=0), "dp", sib_pairs(dp_count))
    g = [got[i * rows:(i + 1) * rows].astype(f32) for i in range(3)]
    own_far, sib_far = lax.optimization_barrier((b[6], got_far))
    q_far = (own_far.astype(f32) + sib_far.astype(f32)).astype(jnp.bfloat16)
    q_self = b[0].astype(f32) + g[0]
    q_up = b[2].astype(f32) + g[1]
    q_dn = b[4].astype(f32) + g[2]
    r_a = lax.ppermute(q_far[:, :half], "dp", dp_pairs(dp_count, 1)).astype(f32)
    r_b = lax.ppermute(q_far[:, half:], "dp", dp_pairs(dp_count, -1)).astype(f32)
    s_a = jnp.concatenate([q_dn[:, :half] + r_a, q_dn[:, half:]], axis=1).astype(jnp.bfloat16)
    s_b = jnp.concatenate([q_up[:, :half], q_up[:, half:] + r_b], axis=1).astype(jnp.bfloat16)
    a_a = lax.ppermute(s_a, "dp", dp_pairs(dp_count, 1)).astype(f32)
    a_b = lax.ppermute(s_b, "dp", dp_pairs(dp_count, -1)).astype(f32)
    return (q_self + a_a + a_b).astype(jnp.bfloat16)


def layer(tokens, chosen, combine_fixed, w_gate, w_up, w_down):
    dp_count = lax.axis_size("dp")
    ex_count = lax.axis_size("expert")
    worker_ordinal = dp_count * ex_count
    tok_count, model_width = tokens.shape
    _, capacity = chosen.shape
    slot_count = min(tok_count, max(4, 2 * capacity // worker_ordinal))
    my_index = lax.axis_index("dp") * ex_count + lax.axis_index("expert")
    owners, is_mine, ranks = slot_tables(chosen, tok_count, my_index)
    local_idx = chosen - owners * tok_count
    matches = is_mine[:, :, None] & (
        ranks[:, :, None] == jnp.arange(slot_count, dtype=jnp.int32)[None, None, :]
    )
    match_int = matches.astype(jnp.int32)
    source_idx = jnp.sum(match_int * local_idx[:, :, None], axis=1)
    present = jnp.sum(match_int, axis=1)
    scaled = combine_fixed.astype(jnp.float32) / 65536.0
    weights = jnp.sum(matches.astype(jnp.float32) * scaled[:, :, None], axis=1)
    send_rows = jnp.take(tokens, source_idx.reshape(-1), axis=0)
    send_rows = jnp.where(present.reshape(-1, 1) > 0, send_rows, jnp.zeros_like(send_rows))
    row_in = lax.all_to_all(send_rows, "expert", split_axis=0, concat_axis=0, tiled=True)
    blocks = gather_dp(row_in, dp_count)
    rows = row_in.shape[0]
    hb = []
    for part in (blocks[:6], blocks[6:7], blocks[7:]):
        picked = jnp.concatenate(part, axis=0)
        gate_act = jnp.dot(picked, w_gate[0], preferred_element_type=jnp.float32)
        up_act = jnp.dot(picked, w_up[0], preferred_element_type=jnp.float32)
        hidden = lax.optimization_barrier((jax.nn.silu(gate_act) * up_act).astype(jnp.bfloat16))
        hb += [hidden[i * rows:(i + 1) * rows] for i in range(len(part))]
    result = [None] * 8
    for group in ((0, 2, 4, 6), (1, 3, 5, 7)):
        out = jnp.dot(
            jnp.concatenate([hb[i] for i in group], axis=0), w_down[0], preferred_element_type=jnp.float32
        ).astype(jnp.bfloat16)
        for n, i in enumerate(group):
            result[i] = out[n * rows:(n + 1) * rows]
    summed = scatter_dp(result, dp_count)
    summed = summed.reshape(ex_count, slot_count, model_width)
    returned = lax.all_to_all(summed, "expert", split_axis=0, concat_axis=0, tiled=True)
    placed = (jnp.arange(tok_count, dtype=jnp.int32)[:, None] == source_idx.reshape(1, -1)) & (
        present.reshape(1, -1) > 0
    )
    mixing = jnp.where(placed, weights.reshape(1, -1), 0.0)
    mix_hi = mixing.astype(jnp.bfloat16)
    mix_lo = (mixing - mix_hi.astype(jnp.float32)).astype(jnp.bfloat16)
    dims = (((1, 2), (0, 1)), ((), ()))
    mix_hi = mix_hi.reshape(tok_count, ex_count, slot_count)
    mix_lo = mix_lo.reshape(tok_count, ex_count, slot_count)
    mixed = lax.dot_general(mix_hi, returned, dims, preferred_element_type=jnp.float32) + lax.dot_general(
        mix_lo, returned, dims, preferred_element_type=jnp.float32
    )
    return mixed.astype(jnp.bfloat16)


def solution(mesh):
    in_specs = (
        P(("dp", "expert"), None),
        P(),
        P(),
        P("expert", None, "dp"),
        P("expert", None, "dp"),
        P("expert", "dp", None),
    )
    out_specs = P(("dp", "expert"), None)
    return jax.shard_map(layer, mesh=mesh, in_specs=in_specs, out_specs=out_specs, check_vma=False)
```

```python
import jax
import jax.numpy as jnp
from jax import lax
from jax.sharding import PartitionSpec as P


def slot_tables(chosen, tok_count, my_index):
    owners = chosen // tok_count
    capacity = chosen.shape[1]
    is_mine = owners == my_index
    earlier = (
        jnp.arange(capacity, dtype=jnp.int32)[:, None]
        < jnp.arange(capacity, dtype=jnp.int32)[None, :]
    ).astype(jnp.bfloat16)
    ranks = jnp.dot(is_mine.astype(jnp.bfloat16), earlier, preferred_element_type=jnp.float32)
    return (owners, is_mine, ranks.astype(jnp.int32))


def dp_pairs(dp_count, shift):
    ny = dp_count // 2
    return [(y * 2 + c, ((y + shift) % ny) * 2 + c) for y in range(ny) for c in range(2)]


def sib_pairs(dp_count):
    return [(y * 2 + c, y * 2 + 1 - c) for y in range(dp_count // 2) for c in range(2)]


def gather_dp(x, dp_count):
    half = x.shape[1] // 2
    up = lax.ppermute(x, "dp", dp_pairs(dp_count, 1))
    dn = lax.ppermute(x, "dp", dp_pairs(dp_count, -1))
    sib = lax.ppermute(x, "dp", sib_pairs(dp_count))
    far_a = lax.ppermute(up[:, :half], "dp", dp_pairs(dp_count, 1))
    far_b = lax.ppermute(dn[:, half:], "dp", dp_pairs(dp_count, -1))
    far = jnp.concatenate([far_a, far_b], axis=1)
    s_up = lax.ppermute(up, "dp", sib_pairs(dp_count))
    s_dn = lax.ppermute(dn, "dp", sib_pairs(dp_count))
    s_far = jnp.concatenate(
        [lax.ppermute(far_a, "dp", sib_pairs(dp_count)), lax.ppermute(far_b, "dp", sib_pairs(dp_count))], axis=1
    )
    return [x, sib, up, s_up, dn, s_dn, far, s_far]


def scatter_dp(p, dp_count):
    rows = p[0].shape[0]
    half = p[0].shape[1] // 2
    f32 = jnp.float32
    b = p
    got_far = lax.ppermute(b[7], "dp", sib_pairs(dp_count))
    got = lax.ppermute(jnp.concatenate([b[1], b[3], b[5]], axis=0), "dp", sib_pairs(dp_count))
    g = [got[i * rows:(i + 1) * rows].astype(f32) for i in range(3)]
    own_far, sib_far = lax.optimization_barrier((b[6], got_far))
    q_far = (own_far.astype(f32) + sib_far.astype(f32)).astype(jnp.bfloat16)
    q_self = b[0].astype(f32) + g[0]
    q_up = b[2].astype(f32) + g[1]
    q_dn = b[4].astype(f32) + g[2]
    r_a = lax.ppermute(q_far[:, :half], "dp", dp_pairs(dp_count, 1)).astype(f32)
    r_b = lax.ppermute(q_far[:, half:], "dp", dp_pairs(dp_count, -1)).astype(f32)
    s_a = jnp.concatenate([q_dn[:, :half] + r_a, q_dn[:, half:]], axis=1).astype(jnp.bfloat16)
    s_b = jnp.concatenate([q_up[:, :half], q_up[:, half:] + r_b], axis=1).astype(jnp.bfloat16)
    a_a = lax.ppermute(s_a, "dp", dp_pairs(dp_count, 1)).astype(f32)
    a_b = lax.ppermute(s_b, "dp", dp_pairs(dp_count, -1)).astype(f32)
    return (q_self + a_a + a_b).astype(jnp.bfloat16)


def layer(tokens, chosen, combine_fixed, w_gate, w_up, w_down):
    dp_count = lax.axis_size("dp")
    ex_count = lax.axis_size("expert")
    worker_ordinal = dp_count * ex_count
    tok_count, model_width = tokens.shape
    _, capacity = chosen.shape
    slot_count = min(tok_count, max(4, 2 * capacity // worker_ordinal))
    my_index = lax.axis_index("dp") * ex_count + lax.axis_index("expert")
    owners, is_mine, ranks = slot_tables(chosen, tok_count, my_index)
    local_idx = chosen - owners * tok_count
    matches = is_mine[:, :, None] & (
        ranks[:, :, None] == jnp.arange(slot_count, dtype=jnp.int32)[None, None, :]
    )
    match_int = matches.astype(jnp.int32)
    source_idx = jnp.sum(match_int * local_idx[:, :, None], axis=1)
    present = jnp.sum(match_int, axis=1)
    scaled = combine_fixed.astype(jnp.float32) / 65536.0
    weights = jnp.sum(matches.astype(jnp.float32) * scaled[:, :, None], axis=1)
    pick = (source_idx.reshape(-1, 1) == jnp.arange(tok_count, dtype=jnp.int32)[None, :]) & (
        present.reshape(-1, 1) > 0
    )
    send_rows = jnp.dot(pick.astype(tokens.dtype), tokens, preferred_element_type=jnp.float32).astype(tokens.dtype)
    row_in = lax.all_to_all(send_rows, "expert", split_axis=0, concat_axis=0, tiled=True)
    blocks = gather_dp(row_in, dp_count)
    rows = row_in.shape[0]
    hidden = []
    for part in (blocks[:6], blocks[6:]):
        picked = jnp.concatenate(part, axis=0)
        gate_act = jnp.dot(picked, w_gate[0], preferred_element_type=jnp.float32)
        up_act = jnp.dot(picked, w_up[0], preferred_element_type=jnp.float32)
        hidden.append((jax.nn.silu(gate_act) * up_act).astype(jnp.bfloat16))
    hidden = lax.optimization_barrier(jnp.concatenate(hidden, axis=0))
    hb = [hidden[i * rows:(i + 1) * rows] for i in range(8)]
    result = [None] * 8
    for group in ((1, 3, 5, 7), (0, 2, 4, 6)):
        out = jnp.dot(
            jnp.concatenate([hb[i] for i in group], axis=0), w_down[0], preferred_element_type=jnp.float32
        ).astype(jnp.bfloat16)
        for n, i in enumerate(group):
            result[i] = out[n * rows:(n + 1) * rows]
    summed = scatter_dp(result, dp_count)
    summed = summed.reshape(ex_count, slot_count, model_width)
    returned = lax.all_to_all(summed, "expert", split_axis=0, concat_axis=0, tiled=True)
    placed = (jnp.arange(tok_count, dtype=jnp.int32)[:, None] == source_idx.reshape(1, -1)) & (
        present.reshape(1, -1) > 0
    )
    mixing = jnp.where(placed, weights.reshape(1, -1), 0.0)
    mix_hi = mixing.astype(jnp.bfloat16)
    mix_lo = (mixing - mix_hi.astype(jnp.float32)).astype(jnp.bfloat16)
    dims = (((1, 2), (0, 1)), ((), ()))
    mix_hi = mix_hi.reshape(tok_count, ex_count, slot_count)
    mix_lo = mix_lo.reshape(tok_count, ex_count, slot_count)
    mixed = lax.dot_general(mix_hi, returned, dims, preferred_element_type=jnp.float32) + lax.dot_general(
        mix_lo, returned, dims, preferred_element_type=jnp.float32
    )
    return mixed.astype(jnp.bfloat16)


def solution(mesh):
    in_specs = (
        P(("dp", "expert"), None),
        P(),
        P(),
        P("expert", None, "dp"),
        P("expert", None, "dp"),
        P("expert", "dp", None),
    )
    out_specs = P(("dp", "expert"), None)
    return jax.shard_map(layer, mesh=mesh, in_specs=in_specs, out_specs=out_specs, check_vma=False)
```

```python
import jax
import jax.numpy as jnp
from jax import lax
from jax.sharding import PartitionSpec as P


def slot_tables(chosen, tok_count, my_index):
    owners = chosen // tok_count
    capacity = chosen.shape[1]
    is_mine = owners == my_index
    earlier = (
        jnp.arange(capacity, dtype=jnp.int32)[:, None]
        < jnp.arange(capacity, dtype=jnp.int32)[None, :]
    ).astype(jnp.bfloat16)
    ranks = jnp.dot(is_mine.astype(jnp.bfloat16), earlier, preferred_element_type=jnp.float32)
    return (owners, is_mine, ranks.astype(jnp.int32))


def dp_pairs(dp_count, shift):
    ny = dp_count // 2
    return [(y * 2 + c, ((y + shift) % ny) * 2 + c) for y in range(ny) for c in range(2)]


def sib_pairs(dp_count):
    return [(y * 2 + c, y * 2 + 1 - c) for y in range(dp_count // 2) for c in range(2)]


def gather_dp(x, dp_count):
    half = x.shape[1] // 2
    up = lax.ppermute(x, "dp", dp_pairs(dp_count, 1))
    dn = lax.ppermute(x, "dp", dp_pairs(dp_count, -1))
    sib = lax.ppermute(x, "dp", sib_pairs(dp_count))
    far_a = lax.ppermute(up[:, :half], "dp", dp_pairs(dp_count, 1))
    far_b = lax.ppermute(dn[:, half:], "dp", dp_pairs(dp_count, -1))
    far = jnp.concatenate([far_a, far_b], axis=1)
    s_up = lax.ppermute(up, "dp", sib_pairs(dp_count))
    s_dn = lax.ppermute(dn, "dp", sib_pairs(dp_count))
    s_far = lax.ppermute(far, "dp", sib_pairs(dp_count))
    return [x, sib, up, s_up, dn, s_dn, far, s_far]


def scatter_dp(p, dp_count):
    rows = p[0].shape[0]
    half = p[0].shape[1] // 2
    f32 = jnp.float32
    b = p
    got_far = lax.ppermute(b[7], "dp", sib_pairs(dp_count))
    got = lax.ppermute(jnp.concatenate([b[1], b[3], b[5]], axis=0), "dp", sib_pairs(dp_count))
    g = [got[i * rows:(i + 1) * rows].astype(f32) for i in range(3)]
    own_far, sib_far = lax.optimization_barrier((b[6], got_far))
    q_far = (own_far.astype(f32) + sib_far.astype(f32)).astype(jnp.bfloat16)
    q_self = b[0].astype(f32) + g[0]
    q_up = b[2].astype(f32) + g[1]
    q_dn = b[4].astype(f32) + g[2]
    r_a = lax.ppermute(q_far[:, :half], "dp", dp_pairs(dp_count, 1)).astype(f32)
    r_b = lax.ppermute(q_far[:, half:], "dp", dp_pairs(dp_count, -1)).astype(f32)
    s_a = jnp.concatenate([q_dn[:, :half] + r_a, q_dn[:, half:]], axis=1).astype(jnp.bfloat16)
    s_b = jnp.concatenate([q_up[:, :half], q_up[:, half:] + r_b], axis=1).astype(jnp.bfloat16)
    a_a = lax.ppermute(s_a, "dp", dp_pairs(dp_count, 1)).astype(f32)
    a_b = lax.ppermute(s_b, "dp", dp_pairs(dp_count, -1)).astype(f32)
    return (q_self + a_a + a_b).astype(jnp.bfloat16)


def layer(tokens, chosen, combine_fixed, w_gate, w_up, w_down):
    dp_count = lax.axis_size("dp")
    ex_count = lax.axis_size("expert")
    worker_ordinal = dp_count * ex_count
    tok_count, model_width = tokens.shape
    _, capacity = chosen.shape
    slot_count = min(tok_count, max(4, 2 * capacity // worker_ordinal))
    my_index = lax.axis_index("dp") * ex_count + lax.axis_index("expert")
    owners, is_mine, ranks = slot_tables(chosen, tok_count, my_index)
    local_idx = chosen - owners * tok_count
    matches = is_mine[:, :, None] & (
        ranks[:, :, None] == jnp.arange(slot_count, dtype=jnp.int32)[None, None, :]
    )
    match_int = matches.astype(jnp.int32)
    source_idx = jnp.sum(match_int * local_idx[:, :, None], axis=1)
    present = jnp.sum(match_int, axis=1)
    scaled = combine_fixed.astype(jnp.float32) / 65536.0
    weights = jnp.sum(matches.astype(jnp.float32) * scaled[:, :, None], axis=1)
    pick = (source_idx.reshape(-1, 1) == jnp.arange(tok_count, dtype=jnp.int32)[None, :]) & (
        present.reshape(-1, 1) > 0
    )
    send_rows = jnp.dot(pick.astype(tokens.dtype), tokens, preferred_element_type=jnp.float32).astype(tokens.dtype)
    row_in = lax.all_to_all(send_rows, "expert", split_axis=0, concat_axis=0, tiled=True)
    blocks = gather_dp(row_in, dp_count)
    rows = row_in.shape[0]
    hidden = []
    for part in (blocks[:6], blocks[6:]):
        picked = jnp.concatenate(part, axis=0)
        gate_act = jnp.dot(picked, w_gate[0], preferred_element_type=jnp.float32)
        up_act = jnp.dot(picked, w_up[0], preferred_element_type=jnp.float32)
        hidden.append((jax.nn.silu(gate_act) * up_act).astype(jnp.bfloat16))
    hidden = jnp.concatenate(hidden, axis=0)
    hb = [hidden[i * rows:(i + 1) * rows] for i in range(8)]
    result = [None] * 8
    for group in ((1, 3, 5, 7), (0, 2, 4, 6)):
        out = jnp.dot(
            jnp.concatenate([hb[i] for i in group], axis=0), w_down[0], preferred_element_type=jnp.float32
        ).astype(jnp.bfloat16)
        for n, i in enumerate(group):
            result[i] = out[n * rows:(n + 1) * rows]
    summed = scatter_dp(result, dp_count)
    summed = summed.reshape(ex_count, slot_count, model_width)
    returned = lax.all_to_all(summed, "expert", split_axis=0, concat_axis=0, tiled=True)
    placed = (jnp.arange(tok_count, dtype=jnp.int32)[:, None] == source_idx.reshape(1, -1)) & (
        present.reshape(1, -1) > 0
    )
    mixing = jnp.where(placed, weights.reshape(1, -1), 0.0)
    mix_hi = mixing.astype(jnp.bfloat16)
    mix_lo = (mixing - mix_hi.astype(jnp.float32)).astype(jnp.bfloat16)
    dims = (((1, 2), (0, 1)), ((), ()))
    mix_hi = mix_hi.reshape(tok_count, ex_count, slot_count)
    mix_lo = mix_lo.reshape(tok_count, ex_count, slot_count)
    mixed = lax.dot_general(mix_hi, returned, dims, preferred_element_type=jnp.float32) + lax.dot_general(
        mix_lo, returned, dims, preferred_element_type=jnp.float32
    )
    return mixed.astype(jnp.bfloat16)


def solution(mesh):
    in_specs = (
        P(("dp", "expert"), None),
        P(),
        P(),
        P("expert", None, "dp"),
        P("expert", None, "dp"),
        P("expert", "dp", None),
    )
    out_specs = P(("dp", "expert"), None)
    return jax.shard_map(layer, mesh=mesh, in_specs=in_specs, out_specs=out_specs, check_vma=False)
```
